256 devices in a mesh: lat: 32 (over x_lo, z, core), lon: 8 (over y, x_hi).
Axes of the slice: x: 4 (x_hi: 2, x_lo: 2; x = x_hi * 2 + x_lo), y: 4, z: 8, core: 2. Of those that a mesh axis runs over, the one named last changes fastest.
Arguments:
- tokens: bfloat16 [4, 192, 96, 512], P(None, 'lat', 'lon'), may hold values from -6 to 6
- w_qkv: bfloat16 [512, 1536], P('lon'), may hold values from -0.25 to 0.25
- w_out: bfloat16 [512, 512], P('lon'), may hold values from -0.25 to 0.25
- gain: float32 [512], replicated, may hold values from 0.1 to 1.9
- tau: float32 [8], replicated, may hold values from 1 to 12
- cotangent: bfloat16 [4, 192, 96, 512], P(None, 'lat', 'lon'), may hold values from -6 to 6
Outputs:
- output: bfloat16 [4, 192, 96, 512], P(None, 'lat', 'lon')
- grad_tokens: bfloat16 [4, 192, 96, 512], P(None, 'lat', 'lon')
- grad_qkv: float32 [512, 1536], P('lon')
- grad_out: float32 [512, 512], P('lon')
The draws below stay inside these ranges and needn't reach their ends.
All inputs are finite; a program needn't handle non-finite values.
Results may differ from the reference program's by a relative error of at most 0.035.
Values may be sent and summed in bfloat16 or wider, within the bound.
No kernel may reach another device: no remote copies, remote signals or barrier semaphores. Data moves between devices by JAX's collectives and lax.ppermute only.
A program may use at most 128 MiB of HBM per device.

```python
import math
import jax
import jax.numpy as jnp
from jax import lax

D = 512
HEADS = 8
LV = 4
WL = 2
WH = 6
WW = 12
HD = 64
KEYS = 288
NH = 192
NW = 96


def with_spikes(values, rng, source, target, blocks, factor):
    owner, partner = [(jnp.arange(values.shape[dim]) // (values.shape[dim] // blocks)).reshape([-1 if axis == dim else 1 for axis in range(values.ndim)]) for dim in (source, target)]
    chosen = jax.random.permutation(rng, blocks)[partner]
    strong = (owner == chosen) | (owner == (partner + blocks // 2) % blocks)
    return jnp.where(strong, factor * values, values)


def shard_levels(own_key, shape, cuts, least, largest):
    factor_of, own = 1.0, jax.random.fold_in(own_key, 6)
    for dim, shards_of in cuts:
        steps = jnp.exp(jax.random.uniform(jax.random.fold_in(own, dim), (shards_of,), jnp.float32, least / len(cuts), largest / len(cuts)))
        factor_of = factor_of * jnp.repeat(steps, shape[dim] // shards_of).reshape([-1 if axis == dim else 1 for axis in range(len(shape))])
    return factor_of


def centred(own_key, shape, scale, bound, shards=(), held_as=jnp.bfloat16):
    array = jax.random.normal(own_key, shape, jnp.float32) * scale
    if len(shards) > 0:
        array = shard_levels(own_key, shape, shards, -0.22, 0.18) * array
    return jnp.clip(array, min=-bound, max=bound).astype(held_as)


def gaussian_with(key, shape, scale, most, pieces, heavy, dtype=jnp.bfloat16):
    result = scale * jax.random.normal(key, shape, jnp.float32)
    if pieces:
        result = result * shard_levels(key, shape, pieces, -0.22, 0.18)
    return jnp.clip(with_spikes(result, jax.random.fold_in(key, 3), *heavy), -most, most).astype(dtype)


def setup_inputs(seed: int = 0) -> dict:
    key_of = jax.random.split(jax.random.key(seed), 7)
    tokens = gaussian_with(key_of[0], (LV, NH, NW, D), 1.0, 6.0, ((1, 32), (2, 8)), (2, 3, 8, 2.0))
    w_qkv = centred(key_of[1], (D, 3 * D), D ** -0.5, 0.25, ((0, 8),))
    w_out = centred(key_of[2], (D, D), D ** -0.5, 0.25, ((0, 8),))
    gain = jnp.clip(1.0 + 0.18 * jax.random.normal(key_of[3], (D,), jnp.float32), 0.1, 1.9)
    tau = jnp.clip(jnp.exp(jax.random.uniform(key_of[4], (HEADS,), jnp.float32, math.log(1.0), math.log(12.0))), 1.0, 12.0)
    cotangent = centred(key_of[5], (LV, NH, NW, D), 1.0, 6.0, ((1, 32), (2, 8)))
    return dict(tokens=tokens, w_qkv=w_qkv, w_out=w_out, gain=gain, tau=tau, cotangent=cotangent)


NORM_EPS = 1e-05
UNIT_EPS = 1e-06

def unit_rows(vectors):
    scaling = lax.rsqrt(lax.optimization_barrier(jnp.sum(vectors * vectors, axis=-1, keepdims=True)) + UNIT_EPS)
    return (vectors * scaling, scaling)

def unit_back(vectors, scaling, gradient):
    inner_sum = lax.optimization_barrier(jnp.sum(vectors * gradient, axis=-1, keepdims=True))
    return scaling * (gradient - vectors * (inner_sum * scaling * scaling))

def norm_forward(y_rows):
    centered = y_rows - lax.optimization_barrier(jnp.mean(y_rows, axis=-1, keepdims=True))
    inverse = lax.rsqrt(lax.optimization_barrier(jnp.mean(centered * centered, axis=-1, keepdims=True)) + NORM_EPS)
    return (centered * inverse, inverse)

def norm_back(normed, inverse, upstream):
    mean_up = lax.optimization_barrier(jnp.mean(upstream, axis=-1, keepdims=True))
    mean_cross = lax.optimization_barrier(jnp.mean(upstream * normed, axis=-1, keepdims=True))
    return inverse * (upstream - mean_up - normed * mean_cross)

def to_windows(field):
    channels = field.shape[-1]
    rolled = jnp.roll(field, WW // 2, axis=2)
    padded = jnp.pad(rolled, ((0, 0), (WH // 2, WH // 2), (0, 0), (0, 0)))
    shaped = padded.reshape(LV, (NH + WH) // WH, WH, NW // WW, WW, channels)
    return shaped.transpose(1, 3, 0, 2, 4, 5).reshape((NH + WH) // WH, NW // WW, KEYS, channels)

def from_windows(windows):
    channels = windows.shape[-1]
    shaped = windows.reshape((NH + WH) // WH, NW // WW, LV, WH, WW, channels)
    padded = shaped.transpose(2, 0, 3, 1, 4, 5).reshape(LV, NH + WH, NW, channels)
    return jnp.roll(padded[:, WH // 2:WH // 2 + NH], -(WW // 2), axis=2)

def window_masks():
    token_ids = jnp.arange(KEYS)
    level_win = (token_ids // (WH * WW) + WL // 2) // WL
    same_level = level_win[:, None] == level_win[None, :]
    win_ids = jnp.arange((NH + WH) // WH)
    padded_row = WH * win_ids[:, None] + token_ids[None, :] // WW % WH
    inside = (padded_row >= WH // 2) & (padded_row < WH // 2 + NH)
    return (same_level[None, :, :] & inside[:, None, :]).astype(jnp.float32)

def reference(tokens, w_qkv, w_out, gain, tau, cotangent):
    flat_tok = tokens.reshape(-1, D)
    projected = jnp.dot(flat_tok, w_qkv, preferred_element_type=jnp.float32).astype(jnp.bfloat16)
    query_f = projected[:, :D].astype(jnp.float32).reshape(-1, HEADS, HD)
    key_f = projected[:, D:2 * D].astype(jnp.float32).reshape(-1, HEADS, HD)
    query_n, query_scale = unit_rows(query_f)
    key_n, key_scale = unit_rows(key_f)
    query_b = query_n.astype(jnp.bfloat16).reshape(LV, NH, NW, D)
    key_b = key_n.astype(jnp.bfloat16).reshape(LV, NH, NW, D)
    value_b = projected[:, 2 * D:].reshape(LV, NH, NW, D)
    win_shape = ((NH + WH) // WH, NW // WW, KEYS, HEADS, HD)
    query_w = to_windows(query_b).reshape(win_shape)
    key_w = to_windows(key_b).reshape(win_shape)
    value_w = to_windows(value_b).reshape(win_shape)
    masks = window_masks()
    temper = tau[:, None, None]

    def attention_probs(q_win, k_win, mask_win):
        scores = jnp.einsum('wqhd,wkhd->whqk', q_win.astype(jnp.float32), k_win.astype(jnp.float32)) * temper
        weights = jnp.exp(scores) * mask_win[None, None]
        return weights / lax.optimization_barrier(jnp.sum(weights, axis=-1, keepdims=True))

    def forward_win(operands):
        q_win, k_win, v_win, mask_win = operands
        probs = attention_probs(q_win, k_win, mask_win)
        probs_b = lax.optimization_barrier(probs.astype(jnp.bfloat16)).astype(jnp.float32)
        mixed = jnp.einsum('whqk,wkhd->wqhd', probs_b, v_win.astype(jnp.float32))
        return mixed.astype(jnp.bfloat16)
    attended_w = lax.map(forward_win, (query_w, key_w, value_w, masks))
    attended = from_windows(attended_w.reshape(win_shape[:3] + (D,))).reshape(-1, D)
    y_rows = jnp.dot(attended, w_out, preferred_element_type=jnp.float32)
    normed, inverse = norm_forward(y_rows)
    output = (flat_tok.astype(jnp.float32) + gain * normed).astype(jnp.bfloat16)
    upstream = gain * cotangent.reshape(-1, D).astype(jnp.float32)
    grad_y = norm_back(normed, inverse, upstream).astype(jnp.bfloat16)
    grad_out = jnp.dot(attended.T, grad_y, preferred_element_type=jnp.float32)
    grad_att = jnp.dot(grad_y, w_out.T, preferred_element_type=jnp.float32).astype(jnp.bfloat16)
    grad_att_w = to_windows(grad_att.reshape(LV, NH, NW, D)).reshape(win_shape)

    def backward_win(operands):
        q_win, k_win, v_win, d_win, mask_win = operands
        probs = attention_probs(q_win, k_win, mask_win)
        probs_b = lax.optimization_barrier(probs.astype(jnp.bfloat16)).astype(jnp.float32)
        grad_f = d_win.astype(jnp.float32)
        dprob = jnp.einsum('wqhd,wkhd->whqk', grad_f, v_win.astype(jnp.float32))
        total_sum = lax.optimization_barrier(jnp.sum(probs * dprob, axis=-1, keepdims=True))
        dscore = temper * (probs * (dprob - total_sum))
        dscore = lax.optimization_barrier(dscore.astype(jnp.bfloat16)).astype(jnp.float32)
        dquery = jnp.einsum('whqk,wkhd->wqhd', dscore, k_win.astype(jnp.float32))
        dkey = jnp.einsum('whqk,wqhd->wkhd', dscore, q_win.astype(jnp.float32))
        dvalue = jnp.einsum('whqk,wqhd->wkhd', probs_b, grad_f)
        return (dquery, dkey, dvalue)
    dquery_w, dkey_w, dvalue_w = lax.map(backward_win, (query_w, key_w, value_w, grad_att_w, masks))
    flat_shape = win_shape[:3] + (D,)
    dquery = from_windows(dquery_w.reshape(flat_shape)).reshape(-1, HEADS, HD)
    dkey = from_windows(dkey_w.reshape(flat_shape)).reshape(-1, HEADS, HD)
    dvalue = from_windows(dvalue_w.reshape(flat_shape)).reshape(-1, D)
    grad_q = unit_back(query_f, query_scale, dquery).reshape(-1, D)
    grad_k = unit_back(key_f, key_scale, dkey).reshape(-1, D)
    grad_proj = jnp.concatenate([grad_q, grad_k, dvalue], axis=1).astype(jnp.bfloat16)
    grad_qkv = jnp.dot(flat_tok.T, grad_proj, preferred_element_type=jnp.float32)
    grad_tok = cotangent.reshape(-1, D).astype(jnp.float32) + jnp.dot(grad_proj, w_qkv.T, preferred_element_type=jnp.float32)
    grad_tokens = grad_tok.astype(jnp.bfloat16).reshape(LV, NH, NW, D)
    return (output.reshape(LV, NH, NW, D), grad_tokens, grad_qkv, grad_out)
```

```python
import jax
import jax.numpy as jnp
from jax import lax
from jax.sharding import PartitionSpec as P

LV = 4
WL = 2
WH = 6
WW = 12
KEYS = 288


NORM_EPS = 1e-05
UNIT_EPS = 1e-06


def with_halo(shard, sides, width, wrap):
    for axis, dim in sides:
        peers, length = (lax.axis_size(axis), shard.shape[dim])
        up = [(i, (i + 1) % peers) for i in range(peers if wrap else peers - 1)]
        down = [(j, i) for i, j in up]
        last = lax.slice_in_dim(shard, length - width, length, axis=dim)
        initial = lax.slice_in_dim(shard, 0, width, axis=dim)
        before = lax.ppermute(last, axis, up)
        after = lax.ppermute(initial, axis, down)
        shard = jnp.concatenate([before, shard, after], axis=dim)
    return shard


def from_behind(block, axis, distance):
    devices = range(lax.axis_size(axis))
    route = [((i - distance) % len(devices), i) for i in devices]
    return lax.ppermute(block, axis, route)


def from_behind_2(block, axis, distance):
    devices = range(lax.axis_size(axis))
    route = [(i - distance, i) for i in devices if i - distance in devices]
    return lax.ppermute(block, axis, route)


def gather_rows(block, axis):
    peers = lax.axis_size(axis)
    copies = jnp.broadcast_to(block[None], (peers,) + block.shape)
    spread = lax.all_to_all(copies, axis, 0, 0, tiled=False)
    return spread.reshape((peers * block.shape[0],) + block.shape[1:])


def sum_rows(partial, axis):
    peers = lax.axis_size(axis)
    chunks = partial.reshape((peers, partial.shape[0] // peers) + partial.shape[1:])
    spread = lax.all_to_all(chunks, axis, 0, 0, tiled=False)
    return jnp.sum(spread.astype(jnp.float32), axis=0)


def sum_everywhere(partial, axis):
    peers = lax.axis_size(axis)
    own = sum_rows(partial, axis).astype(jnp.bfloat16)
    copies = jnp.broadcast_to(own[None], (peers,) + own.shape)
    spread = lax.all_to_all(copies, axis, 0, 0, tiled=False)
    return spread.reshape((peers * own.shape[0],) + own.shape[1:])


def unit_rows(vectors):
    scaling = lax.rsqrt(jnp.sum(vectors * vectors, axis=-1, keepdims=True) + UNIT_EPS)
    return (vectors * scaling, scaling)


def unit_back(vectors, scaling, gradient):
    inner_sum = jnp.sum(vectors * gradient, axis=-1, keepdims=True)
    return scaling * (gradient - vectors * (inner_sum * scaling * scaling))


def norm_forward(y_rows):
    centered = y_rows - jnp.mean(y_rows, axis=-1, keepdims=True)
    inverse = lax.rsqrt(jnp.mean(centered * centered, axis=-1, keepdims=True) + NORM_EPS)
    return (centered * inverse, inverse)


def norm_back(normed, inverse, upstream):
    mean_up = jnp.mean(upstream, axis=-1, keepdims=True)
    mean_cross = jnp.mean(upstream * normed, axis=-1, keepdims=True)
    return inverse * (upstream - mean_up - normed * mean_cross)


def key_windows(extended):
    ext_rows = extended.shape[1]
    ext_cols = extended.shape[2]
    channels = extended.shape[3]
    shaped = extended.reshape(LV, ext_rows // WH, WH, ext_cols // WW, WW, channels)
    return shaped.transpose(1, 3, 0, 2, 4, 5).reshape(
        ext_rows // WH, ext_cols // WW, KEYS, channels
    )


def key_layout(windows):
    win_rows = windows.shape[0]
    win_cols = windows.shape[1]
    channels = windows.shape[3]
    shaped = windows.reshape(win_rows, win_cols, LV, WH, WW, channels)
    return shaped.transpose(2, 0, 3, 1, 4, 5).reshape(LV, win_rows * WH, win_cols * WW, channels)


def query_units(own_grid):
    lat_rows = own_grid.shape[1]
    lon_cols = own_grid.shape[2]
    channels = own_grid.shape[3]
    half_h = WH // 2
    half_w = WW // 2
    shaped = own_grid.reshape(LV, lat_rows // half_h, half_h, lon_cols // half_w, half_w, channels)
    return shaped.transpose(1, 3, 0, 2, 4, 5).reshape(
        lat_rows // half_h, lon_cols // half_w, LV * half_h * half_w, channels
    )


def query_layout(units):
    row_units = units.shape[0]
    col_units = units.shape[1]
    channels = units.shape[3]
    half_h = WH // 2
    half_w = WW // 2
    shaped = units.reshape(row_units, col_units, LV, half_h, half_w, channels)
    return shaped.transpose(2, 0, 3, 1, 4, 5).reshape(
        LV, row_units * half_h, col_units * half_w, channels
    )


def spread_units(blocks, along):
    win_total = blocks.shape[along]
    first_part = lax.slice_in_dim(blocks, 0, 1, axis=along)
    middle_part = jnp.repeat(lax.slice_in_dim(blocks, 1, win_total - 1, axis=along), 2, axis=along)
    last_part = lax.slice_in_dim(blocks, win_total - 1, win_total, axis=along)
    return jnp.concatenate([first_part, middle_part, last_part], axis=along)


def merge_units(units, along):
    unit_total = units.shape[along]
    first_part = lax.slice_in_dim(units, 0, 1, axis=along)
    last_part = lax.slice_in_dim(units, unit_total - 1, unit_total, axis=along)
    middle = lax.slice_in_dim(units, 1, unit_total - 1, axis=along)
    new_shape = middle.shape[:along] + ((unit_total - 2) // 2, 2) + middle.shape[along + 1 :]
    middle_part = jnp.sum(middle.reshape(new_shape), axis=along + 1)
    return jnp.concatenate([first_part, middle_part, last_part], axis=along)


def cross_rows(left_mat, right_mat):
    return lax.dot_general(
        left_mat, right_mat, (((0,), (0,)), ((), ())), preferred_element_type=jnp.float32
    )


def on_device(tokens, w_qkv, w_out, gain, tau, cotangent):
    lat_rows = tokens.shape[1]
    lon_cols = tokens.shape[2]
    model_width = tokens.shape[3]
    head_count = tau.shape[0]
    head_dim = model_width // head_count
    tok_count = LV * lat_rows * lon_cols
    half_h = WH // 2
    half_w = WW // 2
    tok_flat = tokens.reshape(tok_count, model_width)
    src_count = tok_flat.shape[0]
    tok_part = tok_flat
    weights_all = gather_rows(jnp.concatenate([w_qkv, w_out], axis=1), "lon")
    w_qkv_all = weights_all[:, : 3 * model_width]
    w_out_all = weights_all[:, 3 * model_width :]
    projected = jnp.dot(
        tok_part,
        w_qkv_all,
        preferred_element_type=jnp.float32,
    )
    proj_b = projected.astype(jnp.bfloat16)
    query_grid = proj_b[:, :model_width].reshape(LV, lat_rows, lon_cols, model_width)
    query_f = query_grid.astype(jnp.float32).reshape(tok_count, head_count, head_dim)
    key_f = (
        proj_b[:, model_width : 2 * model_width]
        .astype(jnp.float32)
        .reshape(src_count, head_count, head_dim)
    )
    query_n, query_scale = unit_rows(query_f)
    key_n, key_scale = unit_rows(key_f)
    query_b = query_n.astype(jnp.bfloat16).reshape(LV, lat_rows, lon_cols, model_width)
    key_b = key_n.astype(jnp.bfloat16).reshape(src_count, model_width)
    kv_source = jnp.concatenate([key_b, proj_b[:, 2 * model_width :]], axis=1).reshape(
        LV, lat_rows, lon_cols, 2 * model_width
    )
    ext_rows = with_halo(kv_source, (("lat", 1),), half_h, False)
    ext_all = with_halo(ext_rows, (("lon", 2),), half_w, True)
    keys_units = spread_units(spread_units(key_windows(ext_all), 0), 1)
    row_units = keys_units.shape[0]
    col_units = keys_units.shape[1]
    key_u = keys_units[..., :model_width].reshape(row_units, col_units, KEYS, head_count, head_dim)
    value_u = keys_units[..., model_width:].reshape(
        row_units, col_units, KEYS, head_count, head_dim
    )
    query_count = LV * half_h * half_w
    query_u = query_units(query_b).reshape(row_units, col_units, query_count, head_count, head_dim)
    token_ids = jnp.arange(KEYS)
    query_ids = jnp.arange(query_count)
    key_level = (token_ids // (WH * WW) + WL // 2) // WL
    query_level = (query_ids // (half_h * half_w) + WL // 2) // WL
    same_level = query_level[:, None] == key_level[None, :]
    unit_ids = jnp.arange(row_units)
    ext_row = WH * ((unit_ids[:, None] + 1) // 2) + token_ids[None, :] // WW % WH
    global_row = lax.axis_index("lat") * lat_rows - half_h + ext_row
    inside = (global_row >= 0) & (global_row < lat_rows * lax.axis_size("lat"))
    allowed = (same_level[None, :, :] & inside[:, None, :]).astype(jnp.float32)[:, None, None]
    temper = tau[:, None, None]
    scores = (
        jnp.einsum("abqhd,abkhd->abhqk", query_u, key_u, preferred_element_type=jnp.float32)
        * temper
    )
    weights = jnp.exp(scores) * allowed
    probs = weights / jnp.sum(weights, axis=-1, keepdims=True)
    probs_b = probs.astype(jnp.bfloat16)
    mixed = jnp.einsum(
        "abhqk,abkhd->abqhd", probs_b, value_u, preferred_element_type=jnp.float32
    ).astype(jnp.bfloat16)
    attended = query_layout(mixed.reshape(row_units, col_units, query_count, model_width)).reshape(
        tok_count, model_width
    )
    att_part = attended
    y_rows = jnp.dot(
        att_part,
        w_out_all,
        preferred_element_type=jnp.float32,
    )
    normed, inverse = norm_forward(y_rows)
    output = (tok_flat.astype(jnp.float32) + gain * normed).astype(jnp.bfloat16)
    cot_flat = cotangent.reshape(tok_count, model_width).astype(jnp.float32)
    grad_y = norm_back(normed, inverse, gain * cot_flat).astype(jnp.bfloat16)
    grad_att = jnp.dot(
        grad_y,
        w_out_all.T,
        preferred_element_type=jnp.float32,
    )
    grad_att_b = grad_att.astype(jnp.bfloat16).reshape(LV, lat_rows, lon_cols, model_width)
    grad_u = query_units(grad_att_b).reshape(
        row_units, col_units, query_count, head_count, head_dim
    )
    dprob = jnp.einsum("abqhd,abkhd->abhqk", grad_u, value_u, preferred_element_type=jnp.float32)
    total_sum = jnp.sum(probs * dprob, axis=-1, keepdims=True)
    dscore = (temper * (probs * (dprob - total_sum))).astype(jnp.bfloat16)
    dquery = jnp.einsum("abhqk,abkhd->abqhd", dscore, key_u, preferred_element_type=jnp.float32)
    dkey = jnp.einsum("abhqk,abqhd->abkhd", dscore, query_u, preferred_element_type=jnp.float32)
    dvalue = jnp.einsum("abhqk,abqhd->abkhd", probs_b, grad_u, preferred_element_type=jnp.float32)
    key_grads = jnp.concatenate(
        [
            dkey.reshape(row_units, col_units, KEYS, model_width),
            dvalue.reshape(row_units, col_units, KEYS, model_width),
        ],
        axis=3,
    )
    ext_grad = key_layout(merge_units(merge_units(key_grads, 0), 1))
    dquery_own = query_layout(
        dquery.reshape(row_units, col_units, query_count, model_width)
    ).reshape(tok_count, head_count, head_dim)
    grad_q = unit_back(query_f, query_scale, dquery_own).reshape(
        LV, lat_rows, lon_cols, model_width
    )
    west_rim = ext_grad[:, :, :half_w]
    east_rim = ext_grad[:, :, half_w + lon_cols :]
    center = ext_grad[:, :, half_w : half_w + lon_cols]
    from_east = from_behind(west_rim.astype(jnp.bfloat16), "lon", -1).astype(west_rim.dtype)
    from_west = from_behind(east_rim.astype(jnp.bfloat16), "lon", 1).astype(east_rim.dtype)
    center = center.at[:, :, :half_w].add(from_west).at[:, :, lon_cols - half_w :].add(from_east)
    north_rim = center[:, :half_h]
    south_rim = center[:, half_h + lat_rows :]
    middle = center[:, half_h : half_h + lat_rows]
    from_south = from_behind_2(north_rim.astype(jnp.bfloat16), "lat", -1).astype(north_rim.dtype)
    from_north = from_behind_2(south_rim.astype(jnp.bfloat16), "lat", 1).astype(south_rim.dtype)
    middle = middle.at[:, :half_h].add(from_north).at[:, lat_rows - half_h :].add(from_south)
    own_grads = middle.reshape(tok_count, 2 * model_width)
    grad_k = unit_back(
        key_f, key_scale, own_grads[:, :model_width].reshape(tok_count, head_count, head_dim)
    ).reshape(tok_count, model_width)
    grad_q_src = grad_q.reshape(tok_count, model_width)
    dvalue_src = own_grads[:, model_width:]
    grad_proj = jnp.concatenate([grad_q_src, grad_k, dvalue_src], axis=1).astype(jnp.bfloat16)
    grad_in = jnp.dot(
        grad_proj,
        w_qkv_all.T,
        preferred_element_type=jnp.float32,
    )
    grad_tokens = (
        (cot_flat + grad_in).astype(jnp.bfloat16).reshape(LV, lat_rows, lon_cols, model_width)
    )
    tok_part = tok_flat
    att_part = attended
    partial = jnp.concatenate(
        [cross_rows(tok_part, grad_proj), cross_rows(att_part, grad_y)], axis=1
    ).astype(jnp.bfloat16)
    shard_sum = sum_rows(partial, "lon").astype(jnp.bfloat16)
    summed = sum_everywhere(shard_sum, "lat").astype(jnp.float32)
    grad_qkv = summed[:, : 3 * model_width]
    grad_out = summed[:, 3 * model_width :]
    return (output.reshape(LV, lat_rows, lon_cols, model_width), grad_tokens, grad_qkv, grad_out)


def solution(mesh):
    in_specs = (
        P(None, "lat", "lon", None),
        P("lon", None),
        P("lon", None),
        P(),
        P(),
        P(None, "lat", "lon", None),
    )
    out_specs = (
        P(None, "lat", "lon", None),
        P(None, "lat", "lon", None),
        P("lon", None),
        P("lon", None),
    )
    return jax.shard_map(
        on_device, mesh=mesh, in_specs=in_specs, out_specs=out_specs, check_vma=False
    )
```

```python
import jax
import jax.numpy as jnp
from jax import lax
from jax.sharding import PartitionSpec as P

LV = 4
WL = 2
WH = 6
WW = 12
KEYS = 288


NORM_EPS = 1e-05
UNIT_EPS = 1e-06


def with_halo(shard, sides, width, wrap):
    for axis, dim in sides:
        peers, length = (lax.axis_size(axis), shard.shape[dim])
        up = [(i, (i + 1) % peers) for i in range(peers if wrap else peers - 1)]
        down = [(j, i) for i, j in up]
        last = lax.slice_in_dim(shard, length - width, length, axis=dim)
        initial = lax.slice_in_dim(shard, 0, width, axis=dim)
        before = lax.ppermute(last, axis, up)
        after = lax.ppermute(initial, axis, down)
        shard = jnp.concatenate([before, shard, after], axis=dim)
    return shard


def from_behind(block, axis, distance):
    devices = range(lax.axis_size(axis))
    route = [((i - distance) % len(devices), i) for i in devices]
    return lax.ppermute(block, axis, route)


def from_behind_2(block, axis, distance):
    devices = range(lax.axis_size(axis))
    route = [(i - distance, i) for i in devices if i - distance in devices]
    return lax.ppermute(block, axis, route)


def gather_rows(block, axis):
    peers = lax.axis_size(axis)
    copies = jnp.broadcast_to(block[None], (peers,) + block.shape)
    spread = lax.all_to_all(copies, axis, 0, 0, tiled=False)
    return spread.reshape((peers * block.shape[0],) + block.shape[1:])


def sum_rows(partial, axis):
    peers = lax.axis_size(axis)
    chunks = partial.reshape((peers, partial.shape[0] // peers) + partial.shape[1:])
    spread = lax.all_to_all(chunks, axis, 0, 0, tiled=False)
    return jnp.sum(spread.astype(jnp.float32), axis=0)


def sum_everywhere(partial, axis):
    peers = lax.axis_size(axis)
    own = sum_rows(partial, axis).astype(jnp.bfloat16)
    copies = jnp.broadcast_to(own[None], (peers,) + own.shape)
    spread = lax.all_to_all(copies, axis, 0, 0, tiled=False)
    return spread.reshape((peers * own.shape[0],) + own.shape[1:])


def unit_rows(vectors):
    scaling = lax.rsqrt(jnp.sum(vectors * vectors, axis=-1, keepdims=True) + UNIT_EPS)
    return (vectors * scaling, scaling)


def unit_back(vectors, scaling, gradient):
    inner_sum = jnp.sum(vectors * gradient, axis=-1, keepdims=True)
    return scaling * (gradient - vectors * (inner_sum * scaling * scaling))


def norm_forward(y_rows):
    centered = y_rows - jnp.mean(y_rows, axis=-1, keepdims=True)
    inverse = lax.rsqrt(jnp.mean(centered * centered, axis=-1, keepdims=True) + NORM_EPS)
    return (centered * inverse, inverse)


def norm_back(normed, inverse, upstream):
    mean_up = jnp.mean(upstream, axis=-1, keepdims=True)
    mean_cross = jnp.mean(upstream * normed, axis=-1, keepdims=True)
    return inverse * (upstream - mean_up - normed * mean_cross)


def key_windows(extended):
    ext_rows = extended.shape[1]
    ext_cols = extended.shape[2]
    channels = extended.shape[3]
    shaped = extended.reshape(LV, ext_rows // WH, WH, ext_cols // WW, WW, channels)
    return shaped.transpose(1, 3, 0, 2, 4, 5).reshape(
        ext_rows // WH, ext_cols // WW, KEYS, channels
    )


def key_layout(windows):
    win_rows = windows.shape[0]
    win_cols = windows.shape[1]
    channels = windows.shape[3]
    shaped = windows.reshape(win_rows, win_cols, LV, WH, WW, channels)
    return shaped.transpose(2, 0, 3, 1, 4, 5).reshape(LV, win_rows * WH, win_cols * WW, channels)


def query_units(own_grid):
    lat_rows = own_grid.shape[1]
    lon_cols = own_grid.shape[2]
    channels = own_grid.shape[3]
    half_h = WH // 2
    half_w = WW // 2
    shaped = own_grid.reshape(LV, lat_rows // half_h, half_h, lon_cols // half_w, half_w, channels)
    return shaped.transpose(1, 3, 0, 2, 4, 5).reshape(
        lat_rows // half_h, lon_cols // half_w, LV * half_h * half_w, channels
    )


def query_layout(units):
    row_units = units.shape[0]
    col_units = units.shape[1]
    channels = units.shape[3]
    half_h = WH // 2
    half_w = WW // 2
    shaped = units.reshape(row_units, col_units, LV, half_h, half_w, channels)
    return shaped.transpose(2, 0, 3, 1, 4, 5).reshape(
        LV, row_units * half_h, col_units * half_w, channels
    )


def spread_units(blocks, along):
    win_total = blocks.shape[along]
    first_part = lax.slice_in_dim(blocks, 0, 1, axis=along)
    middle_part = jnp.repeat(lax.slice_in_dim(blocks, 1, win_total - 1, axis=along), 2, axis=along)
    last_part = lax.slice_in_dim(blocks, win_total - 1, win_total, axis=along)
    return jnp.concatenate([first_part, middle_part, last_part], axis=along)


def merge_units(units, along):
    unit_total = units.shape[along]
    first_part = lax.slice_in_dim(units, 0, 1, axis=along)
    last_part = lax.slice_in_dim(units, unit_total - 1, unit_total, axis=along)
    middle = lax.slice_in_dim(units, 1, unit_total - 1, axis=along)
    new_shape = middle.shape[:along] + ((unit_total - 2) // 2, 2) + middle.shape[along + 1 :]
    middle_part = jnp.sum(middle.reshape(new_shape), axis=along + 1)
    return jnp.concatenate([first_part, middle_part, last_part], axis=along)


def cross_rows(left_mat, right_mat):
    return lax.dot_general(
        left_mat, right_mat, (((0,), (0,)), ((), ())), preferred_element_type=jnp.float32
    )


def on_device(tokens, w_qkv, w_out, gain, tau, cotangent):
    lat_rows = tokens.shape[1]
    lon_cols = tokens.shape[2]
    model_width = tokens.shape[3]
    head_count = tau.shape[0]
    head_dim = model_width // head_count
    tok_count = LV * lat_rows * lon_cols
    half_h = WH // 2
    half_w = WW // 2
    tok_flat = tokens.reshape(tok_count, model_width)
    src_count = tok_flat.shape[0]
    tok_part = tok_flat
    weights_all = gather_rows(jnp.concatenate([w_qkv, w_out], axis=1), "lon")
    w_qkv_all = weights_all[:, : 3 * model_width]
    w_out_all = weights_all[:, 3 * model_width :]
    projected = jnp.dot(
        tok_part,
        w_qkv_all,
        preferred_element_type=jnp.float32,
    )
    proj_b = projected.astype(jnp.bfloat16)
    query_grid = proj_b[:, :model_width].reshape(LV, lat_rows, lon_cols, model_width)
    query_f = query_grid.astype(jnp.float32).reshape(tok_count, head_count, head_dim)
    key_f = (
        proj_b[:, model_width : 2 * model_width]
        .astype(jnp.float32)
        .reshape(src_count, head_count, head_dim)
    )
    query_n, query_scale = unit_rows(query_f)
    key_n, key_scale = unit_rows(key_f)
    query_b = query_n.astype(jnp.bfloat16).reshape(LV, lat_rows, lon_cols, model_width)
    key_b = key_n.astype(jnp.bfloat16).reshape(src_count, model_width)
    kv_source = jnp.concatenate([key_b, proj_b[:, 2 * model_width :]], axis=1).reshape(
        LV, lat_rows, lon_cols, 2 * model_width
    )
    ext_rows = with_halo(kv_source, (("lat", 1),), half_h, False)
    ext_all = with_halo(ext_rows, (("lon", 2),), half_w, True)
    keys_units = spread_units(spread_units(key_windows(ext_all), 0), 1)
    row_units = keys_units.shape[0]
    col_units = keys_units.shape[1]
    key_u = keys_units[..., :model_width].reshape(row_units, col_units, KEYS, head_count, head_dim)
    value_u = keys_units[..., model_width:].reshape(
        row_units, col_units, KEYS, head_count, head_dim
    )
    pair_count = row_units * col_units * head_count
    key_u = key_u.transpose(0, 1, 3, 2, 4).reshape(pair_count, KEYS, head_dim)
    value_u = value_u.transpose(0, 1, 3, 2, 4).reshape(pair_count, KEYS, head_dim)
    query_count = LV * half_h * half_w
    query_u = query_units(query_b).reshape(row_units, col_units, query_count, head_count, head_dim)
    query_u = query_u.transpose(0, 1, 3, 2, 4).reshape(pair_count, query_count, head_dim)
    token_ids = jnp.arange(KEYS)
    query_ids = jnp.arange(query_count)
    key_level = (token_ids // (WH * WW) + WL // 2) // WL
    query_level = (query_ids // (half_h * half_w) + WL // 2) // WL
    same_level = query_level[:, None] == key_level[None, :]
    unit_ids = jnp.arange(row_units)
    ext_row = WH * ((unit_ids[:, None] + 1) // 2) + token_ids[None, :] // WW % WH
    global_row = lax.axis_index("lat") * lat_rows - half_h + ext_row
    inside = (global_row >= 0) & (global_row < lat_rows * lax.axis_size("lat"))
    allowed = (same_level[None, :, :] & inside[:, None, :]).astype(jnp.float32)[:, None, None]
    allowed = jnp.broadcast_to(
        allowed, (row_units, col_units, head_count, query_count, KEYS)
    ).reshape(pair_count, query_count, KEYS)
    temper = jnp.tile(tau, row_units * col_units)[:, None, None]
    scores = (
        jnp.einsum("pqd,pkd->pqk", query_u, key_u, preferred_element_type=jnp.float32)
        * temper
    )
    weights = jnp.exp(scores) * allowed
    probs = weights / jnp.sum(weights, axis=-1, keepdims=True)
    probs_b = probs.astype(jnp.bfloat16)
    mixed = jnp.einsum(
        "pqk,pkd->pqd", probs_b, value_u, preferred_element_type=jnp.float32
    ).astype(jnp.bfloat16)
    mixed = mixed.reshape(row_units, col_units, head_count, query_count, head_dim).transpose(
        0, 1, 3, 2, 4
    )
    attended = query_layout(mixed.reshape(row_units, col_units, query_count, model_width)).reshape(
        tok_count, model_width
    )
    att_part = attended
    y_rows = jnp.dot(
        att_part,
        w_out_all,
        preferred_element_type=jnp.float32,
    )
    normed, inverse = norm_forward(y_rows)
    output = (tok_flat.astype(jnp.float32) + gain * normed).astype(jnp.bfloat16)
    cot_flat = cotangent.reshape(tok_count, model_width).astype(jnp.float32)
    grad_y = norm_back(normed, inverse, gain * cot_flat).astype(jnp.bfloat16)
    grad_att = jnp.dot(
        grad_y,
        w_out_all.T,
        preferred_element_type=jnp.float32,
    )
    grad_att_b = grad_att.astype(jnp.bfloat16).reshape(LV, lat_rows, lon_cols, model_width)
    grad_u = query_units(grad_att_b).reshape(
        row_units, col_units, query_count, head_count, head_dim
    ).transpose(0, 1, 3, 2, 4).reshape(pair_count, query_count, head_dim)
    dprob = jnp.einsum("pqd,pkd->pqk", grad_u, value_u, preferred_element_type=jnp.float32)
    total_sum = jnp.sum(probs * dprob, axis=-1, keepdims=True)
    dscore = (temper * (probs * (dprob - total_sum))).astype(jnp.bfloat16)
    dquery = jnp.einsum("pqk,pkd->pqd", dscore, key_u, preferred_element_type=jnp.float32)
    dkey = jnp.einsum("pqk,pqd->pkd", dscore, query_u, preferred_element_type=jnp.float32)
    dvalue = jnp.einsum("pqk,pqd->pkd", probs_b, grad_u, preferred_element_type=jnp.float32)
    dquery = dquery.reshape(row_units, col_units, head_count, query_count, head_dim).transpose(
        0, 1, 3, 2, 4
    )
    dkey = dkey.reshape(row_units, col_units, head_count, KEYS, head_dim).transpose(0, 1, 3, 2, 4)
    dvalue = dvalue.reshape(row_units, col_units, head_count, KEYS, head_dim).transpose(
        0, 1, 3, 2, 4
    )
    key_grads = jnp.concatenate(
        [
            dkey.reshape(row_units, col_units, KEYS, model_width),
            dvalue.reshape(row_units, col_units, KEYS, model_width),
        ],
        axis=3,
    )
    ext_grad = key_layout(merge_units(merge_units(key_grads, 0), 1))
    dquery_own = query_layout(
        dquery.reshape(row_units, col_units, query_count, model_width)
    ).reshape(tok_count, head_count, head_dim)
    grad_q = unit_back(query_f, query_scale, dquery_own).reshape(
        LV, lat_rows, lon_cols, model_width
    )
    west_rim = ext_grad[:, :, :half_w]
    east_rim = ext_grad[:, :, half_w + lon_cols :]
    center = ext_grad[:, :, half_w : half_w + lon_cols]
    from_east = from_behind(west_rim.astype(jnp.bfloat16), "lon", -1).astype(west_rim.dtype)
    from_west = from_behind(east_rim.astype(jnp.bfloat16), "lon", 1).astype(east_rim.dtype)
    center = center.at[:, :, :half_w].add(from_west).at[:, :, lon_cols - half_w :].add(from_east)
    north_rim = center[:, :half_h]
    south_rim = center[:, half_h + lat_rows :]
    middle = center[:, half_h : half_h + lat_rows]
    from_south = from_behind_2(north_rim.astype(jnp.bfloat16), "lat", -1).astype(north_rim.dtype)
    from_north = from_behind_2(south_rim.astype(jnp.bfloat16), "lat", 1).astype(south_rim.dtype)
    middle = middle.at[:, :half_h].add(from_north).at[:, lat_rows - half_h :].add(from_south)
    own_grads = middle.reshape(tok_count, 2 * model_width)
    grad_k = unit_back(
        key_f, key_scale, own_grads[:, :model_width].reshape(tok_count, head_count, head_dim)
    ).reshape(tok_count, model_width)
    grad_q_src = grad_q.reshape(tok_count, model_width)
    dvalue_src = own_grads[:, model_width:]
    grad_proj = jnp.concatenate([grad_q_src, grad_k, dvalue_src], axis=1).astype(jnp.bfloat16)
    grad_in = jnp.dot(
        grad_proj,
        w_qkv_all.T,
        preferred_element_type=jnp.float32,
    )
    grad_tokens = (
        (cot_flat + grad_in).astype(jnp.bfloat16).reshape(LV, lat_rows, lon_cols, model_width)
    )
    tok_part = tok_flat
    att_part = attended
    partial = jnp.concatenate(
        [cross_rows(tok_part, grad_proj), cross_rows(att_part, grad_y)], axis=1
    ).astype(jnp.bfloat16)
    shard_sum = sum_rows(partial, "lon").astype(jnp.bfloat16)
    summed = sum_everywhere(shard_sum, "lat").astype(jnp.float32)
    grad_qkv = summed[:, : 3 * model_width]
    grad_out = summed[:, 3 * model_width :]
    return (output.reshape(LV, lat_rows, lon_cols, model_width), grad_tokens, grad_qkv, grad_out)


def solution(mesh):
    in_specs = (
        P(None, "lat", "lon", None),
        P("lon", None),
        P("lon", None),
        P(),
        P(),
        P(None, "lat", "lon", None),
    )
    out_specs = (
        P(None, "lat", "lon", None),
        P(None, "lat", "lon", None),
        P("lon", None),
        P("lon", None),
    )
    return jax.shard_map(
        on_device, mesh=mesh, in_specs=in_specs, out_specs=out_specs, check_vma=False
    )
```

```python
import jax
import jax.numpy as jnp
from jax import lax
from jax.sharding import PartitionSpec as P
from jax.experimental import pallas as pl
from jax.experimental.pallas import tpu as pltpu

LV = 4
WL = 2
WH = 6
WW = 12
KEYS = 288


NORM_EPS = 1e-05
UNIT_EPS = 1e-06
HEADS_K = 8
HD_K = 64


def _nt(a, b):
    return lax.dot_general(a, b, (((1,), (1,)), ((), ())), preferred_element_type=jnp.float32)


def _tn(a, b):
    return lax.dot_general(a, b, (((0,), (0,)), ((), ())), preferred_element_type=jnp.float32)


def _probs(tau_ref, head, q_ref, kv_ref, mask):
    lanes = pl.ds(head * HD_K, HD_K)
    scores = _nt(q_ref[0, :, lanes], kv_ref[0, :, lanes]) * tau_ref[head]
    weights = jnp.exp(scores) * mask
    return weights / jnp.sum(weights, axis=-1, keepdims=True)


def attn_fwd_kernel(tau_ref, q_ref, kv_ref, mask_ref, out_ref):
    mask = mask_ref[0]
    width = q_ref.shape[2]
    for head in range(HEADS_K):
        probs = _probs(tau_ref, head, q_ref, kv_ref, mask)
        values = kv_ref[0, :, pl.ds(width + head * HD_K, HD_K)]
        mixed = jnp.dot(probs.astype(jnp.bfloat16), values, preferred_element_type=jnp.float32)
        out_ref[0, :, pl.ds(head * HD_K, HD_K)] = mixed


def attn_bwd_kernel(tau_ref, q_ref, kv_ref, g_ref, mask_ref, dq_ref, dkv_ref):
    mask = mask_ref[0]
    width = q_ref.shape[2]
    for head in range(HEADS_K):
        lanes = pl.ds(head * HD_K, HD_K)
        value_lanes = pl.ds(width + head * HD_K, HD_K)
        probs = _probs(tau_ref, head, q_ref, kv_ref, mask)
        grad = g_ref[0, :, lanes]
        dprob = _nt(grad, kv_ref[0, :, value_lanes])
        total = jnp.sum(probs * dprob, axis=-1, keepdims=True)
        dscore = (tau_ref[head] * (probs * (dprob - total))).astype(jnp.bfloat16)
        dq_ref[0, :, lanes] = jnp.dot(dscore, kv_ref[0, :, lanes], preferred_element_type=jnp.float32)
        dkv_ref[0, :, lanes] = _tn(dscore, q_ref[0, :, lanes])
        dkv_ref[0, :, value_lanes] = _tn(probs.astype(jnp.bfloat16), grad)


def window_fwd(tau, query, kv, mask):
    units, queries, width = query.shape
    keys = kv.shape[1]
    return pl.pallas_call(
        attn_fwd_kernel,
        grid=(units,),
        in_specs=[
            pl.BlockSpec(memory_space=pltpu.SMEM),
            pl.BlockSpec((1, queries, width), lambda u: (u, 0, 0)),
            pl.BlockSpec((1, keys, 2 * width), lambda u: (u, 0, 0)),
            pl.BlockSpec((1, queries, keys), lambda u: (u, 0, 0)),
        ],
        out_specs=pl.BlockSpec((1, queries, width), lambda u: (u, 0, 0)),
        out_shape=jax.ShapeDtypeStruct((units, queries, width), jnp.float32),
    )(tau, query, kv, mask)


def window_bwd(tau, query, kv, grad, mask):
    units, queries, width = query.shape
    keys = kv.shape[1]
    return pl.pallas_call(
        attn_bwd_kernel,
        grid=(units,),
        in_specs=[
            pl.BlockSpec(memory_space=pltpu.SMEM),
            pl.BlockSpec((1, queries, width), lambda u: (u, 0, 0)),
            pl.BlockSpec((1, keys, 2 * width), lambda u: (u, 0, 0)),
            pl.BlockSpec((1, queries, width), lambda u: (u, 0, 0)),
            pl.BlockSpec((1, queries, keys), lambda u: (u, 0, 0)),
        ],
        out_specs=[
            pl.BlockSpec((1, queries, width), lambda u: (u, 0, 0)),
            pl.BlockSpec((1, keys, 2 * width), lambda u: (u, 0, 0)),
        ],
        out_shape=[
            jax.ShapeDtypeStruct((units, queries, width), jnp.float32),
            jax.ShapeDtypeStruct((units, keys, 2 * width), jnp.float32),
        ],
    )(tau, query, kv, grad, mask)


def with_halo(shard, sides, width, wrap):
    for axis, dim in sides:
        peers, length = (lax.axis_size(axis), shard.shape[dim])
        up = [(i, (i + 1) % peers) for i in range(peers if wrap else peers - 1)]
        down = [(j, i) for i, j in up]
        last = lax.slice_in_dim(shard, length - width, length, axis=dim)
        initial = lax.slice_in_dim(shard, 0, width, axis=dim)
        before = lax.ppermute(last, axis, up)
        after = lax.ppermute(initial, axis, down)
        shard = jnp.concatenate([before, shard, after], axis=dim)
    return shard


def from_behind(block, axis, distance):
    devices = range(lax.axis_size(axis))
    route = [((i - distance) % len(devices), i) for i in devices]
    return lax.ppermute(block, axis, route)


def from_behind_2(block, axis, distance):
    devices = range(lax.axis_size(axis))
    route = [(i - distance, i) for i in devices if i - distance in devices]
    return lax.ppermute(block, axis, route)


def gather_rows(block, axis):
    peers = lax.axis_size(axis)
    copies = jnp.broadcast_to(block[None], (peers,) + block.shape)
    spread = lax.all_to_all(copies, axis, 0, 0, tiled=False)
    return spread.reshape((peers * block.shape[0],) + block.shape[1:])


def sum_rows(partial, axis):
    peers = lax.axis_size(axis)
    chunks = partial.reshape((peers, partial.shape[0] // peers) + partial.shape[1:])
    spread = lax.all_to_all(chunks, axis, 0, 0, tiled=False)
    return jnp.sum(spread.astype(jnp.float32), axis=0)


def sum_everywhere(partial, axis):
    peers = lax.axis_size(axis)
    own = sum_rows(partial, axis).astype(jnp.bfloat16)
    copies = jnp.broadcast_to(own[None], (peers,) + own.shape)
    spread = lax.all_to_all(copies, axis, 0, 0, tiled=False)
    return spread.reshape((peers * own.shape[0],) + own.shape[1:])


def unit_rows(vectors):
    scaling = lax.rsqrt(jnp.sum(vectors * vectors, axis=-1, keepdims=True) + UNIT_EPS)
    return (vectors * scaling, scaling)


def unit_back(vectors, scaling, gradient):
    inner_sum = jnp.sum(vectors * gradient, axis=-1, keepdims=True)
    return scaling * (gradient - vectors * (inner_sum * scaling * scaling))


def norm_forward(y_rows):
    centered = y_rows - jnp.mean(y_rows, axis=-1, keepdims=True)
    inverse = lax.rsqrt(jnp.mean(centered * centered, axis=-1, keepdims=True) + NORM_EPS)
    return (centered * inverse, inverse)


def norm_back(normed, inverse, upstream):
    mean_up = jnp.mean(upstream, axis=-1, keepdims=True)
    mean_cross = jnp.mean(upstream * normed, axis=-1, keepdims=True)
    return inverse * (upstream - mean_up - normed * mean_cross)


def key_windows(extended):
    ext_rows = extended.shape[1]
    ext_cols = extended.shape[2]
    channels = extended.shape[3]
    shaped = extended.reshape(LV, ext_rows // WH, WH, ext_cols // WW, WW, channels)
    return shaped.transpose(1, 3, 0, 2, 4, 5).reshape(
        ext_rows // WH, ext_cols // WW, KEYS, channels
    )


def key_layout(windows):
    win_rows = windows.shape[0]
    win_cols = windows.shape[1]
    channels = windows.shape[3]
    shaped = windows.reshape(win_rows, win_cols, LV, WH, WW, channels)
    return shaped.transpose(2, 0, 3, 1, 4, 5).reshape(LV, win_rows * WH, win_cols * WW, channels)


def query_units(own_grid):
    lat_rows = own_grid.shape[1]
    lon_cols = own_grid.shape[2]
    channels = own_grid.shape[3]
    half_h = WH // 2
    half_w = WW // 2
    shaped = own_grid.reshape(LV, lat_rows // half_h, half_h, lon_cols // half_w, half_w, channels)
    return shaped.transpose(1, 3, 0, 2, 4, 5).reshape(
        lat_rows // half_h, lon_cols // half_w, LV * half_h * half_w, channels
    )


def query_layout(units):
    row_units = units.shape[0]
    col_units = units.shape[1]
    channels = units.shape[3]
    half_h = WH // 2
    half_w = WW // 2
    shaped = units.reshape(row_units, col_units, LV, half_h, half_w, channels)
    return shaped.transpose(2, 0, 3, 1, 4, 5).reshape(
        LV, row_units * half_h, col_units * half_w, channels
    )


def spread_units(blocks, along):
    win_total = blocks.shape[along]
    first_part = lax.slice_in_dim(blocks, 0, 1, axis=along)
    middle_part = jnp.repeat(lax.slice_in_dim(blocks, 1, win_total - 1, axis=along), 2, axis=along)
    last_part = lax.slice_in_dim(blocks, win_total - 1, win_total, axis=along)
    return jnp.concatenate([first_part, middle_part, last_part], axis=along)


def merge_units(units, along):
    unit_total = units.shape[along]
    first_part = lax.slice_in_dim(units, 0, 1, axis=along)
    last_part = lax.slice_in_dim(units, unit_total - 1, unit_total, axis=along)
    middle = lax.slice_in_dim(units, 1, unit_total - 1, axis=along)
    new_shape = middle.shape[:along] + ((unit_total - 2) // 2, 2) + middle.shape[along + 1 :]
    middle_part = jnp.sum(middle.reshape(new_shape), axis=along + 1)
    return jnp.concatenate([first_part, middle_part, last_part], axis=along)


def cross_rows(left_mat, right_mat):
    return lax.dot_general(
        left_mat, right_mat, (((0,), (0,)), ((), ())), preferred_element_type=jnp.float32
    )


def on_device(tokens, w_qkv, w_out, gain, tau, cotangent):
    lat_rows = tokens.shape[1]
    lon_cols = tokens.shape[2]
    model_width = tokens.shape[3]
    head_count = tau.shape[0]
    head_dim = model_width // head_count
    tok_count = LV * lat_rows * lon_cols
    half_h = WH // 2
    half_w = WW // 2
    tok_flat = tokens.reshape(tok_count, model_width)
    src_count = tok_flat.shape[0]
    tok_part = tok_flat
    weights_all = gather_rows(jnp.concatenate([w_qkv, w_out], axis=1), "lon")
    w_qkv_all = weights_all[:, : 3 * model_width]
    w_out_all = weights_all[:, 3 * model_width :]
    projected = jnp.dot(
        tok_part,
        w_qkv_all,
        preferred_element_type=jnp.float32,
    )
    proj_b = projected.astype(jnp.bfloat16)
    query_grid = proj_b[:, :model_width].reshape(LV, lat_rows, lon_cols, model_width)
    query_f = query_grid.astype(jnp.float32).reshape(tok_count, head_count, head_dim)
    key_f = (
        proj_b[:, model_width : 2 * model_width]
        .astype(jnp.float32)
        .reshape(src_count, head_count, head_dim)
    )
    query_n, query_scale = unit_rows(query_f)
    key_n, key_scale = unit_rows(key_f)
    query_b = query_n.astype(jnp.bfloat16).reshape(LV, lat_rows, lon_cols, model_width)
    key_b = key_n.astype(jnp.bfloat16).reshape(src_count, model_width)
    kv_source = jnp.concatenate([key_b, proj_b[:, 2 * model_width :]], axis=1).reshape(
        LV, lat_rows, lon_cols, 2 * model_width
    )
    ext_rows = with_halo(kv_source, (("lat", 1),), half_h, False)
    ext_all = with_halo(ext_rows, (("lon", 2),), half_w, True)
    keys_units = spread_units(spread_units(key_windows(ext_all), 0), 1)
    row_units = keys_units.shape[0]
    col_units = keys_units.shape[1]
    unit_count = row_units * col_units
    kv_u = keys_units.reshape(unit_count, KEYS, 2 * model_width)
    query_count = LV * half_h * half_w
    query_u = query_units(query_b).reshape(unit_count, query_count, model_width)
    token_ids = jnp.arange(KEYS)
    query_ids = jnp.arange(query_count)
    key_level = (token_ids // (WH * WW) + WL // 2) // WL
    query_level = (query_ids // (half_h * half_w) + WL // 2) // WL
    same_level = query_level[:, None] == key_level[None, :]
    unit_ids = jnp.arange(row_units)
    ext_row = WH * ((unit_ids[:, None] + 1) // 2) + token_ids[None, :] // WW % WH
    global_row = lax.axis_index("lat") * lat_rows - half_h + ext_row
    inside = (global_row >= 0) & (global_row < lat_rows * lax.axis_size("lat"))
    allowed = (same_level[None, :, :] & inside[:, None, :]).astype(jnp.float32)[:, None]
    allowed = jnp.broadcast_to(allowed, (row_units, col_units, query_count, KEYS)).reshape(
        unit_count, query_count, KEYS
    )
    mixed = window_fwd(tau, query_u, kv_u, allowed).astype(jnp.bfloat16)
    attended = query_layout(mixed.reshape(row_units, col_units, query_count, model_width)).reshape(
        tok_count, model_width
    )
    att_part = attended
    y_rows = jnp.dot(
        att_part,
        w_out_all,
        preferred_element_type=jnp.float32,
    )
    normed, inverse = norm_forward(y_rows)
    output = (tok_flat.astype(jnp.float32) + gain * normed).astype(jnp.bfloat16)
    cot_flat = cotangent.reshape(tok_count, model_width).astype(jnp.float32)
    grad_y = norm_back(normed, inverse, gain * cot_flat).astype(jnp.bfloat16)
    grad_att = jnp.dot(
        grad_y,
        w_out_all.T,
        preferred_element_type=jnp.float32,
    )
    grad_att_b = grad_att.astype(jnp.bfloat16).reshape(LV, lat_rows, lon_cols, model_width)
    grad_u = query_units(grad_att_b).reshape(unit_count, query_count, model_width)
    dquery, key_grads = window_bwd(tau, query_u, kv_u, grad_u, allowed)
    key_grads = key_grads.reshape(row_units, col_units, KEYS, 2 * model_width)
    ext_grad = key_layout(merge_units(merge_units(key_grads, 0), 1))
    dquery_own = query_layout(
        dquery.reshape(row_units, col_units, query_count, model_width)
    ).reshape(tok_count, head_count, head_dim)
    grad_q = unit_back(query_f, query_scale, dquery_own).reshape(
        LV, lat_rows, lon_cols, model_width
    )
    west_rim = ext_grad[:, :, :half_w]
    east_rim = ext_grad[:, :, half_w + lon_cols :]
    center = ext_grad[:, :, half_w : half_w + lon_cols]
    from_east = from_behind(west_rim.astype(jnp.bfloat16), "lon", -1).astype(west_rim.dtype)
    from_west = from_behind(east_rim.astype(jnp.bfloat16), "lon", 1).astype(east_rim.dtype)
    center = center.at[:, :, :half_w].add(from_west).at[:, :, lon_cols - half_w :].add(from_east)
    north_rim = center[:, :half_h]
    south_rim = center[:, half_h + lat_rows :]
    middle = center[:, half_h : half_h + lat_rows]
    from_south = from_behind_2(north_rim.astype(jnp.bfloat16), "lat", -1).astype(north_rim.dtype)
    from_north = from_behind_2(south_rim.astype(jnp.bfloat16), "lat", 1).astype(south_rim.dtype)
    middle = middle.at[:, :half_h].add(from_north).at[:, lat_rows - half_h :].add(from_south)
    own_grads = middle.reshape(tok_count, 2 * model_width)
    grad_k = unit_back(
        key_f, key_scale, own_grads[:, :model_width].reshape(tok_count, head_count, head_dim)
    ).reshape(tok_count, model_width)
    grad_q_src = grad_q.reshape(tok_count, model_width)
    dvalue_src = own_grads[:, model_width:]
    grad_proj = jnp.concatenate([grad_q_src, grad_k, dvalue_src], axis=1).astype(jnp.bfloat16)
    grad_in = jnp.dot(
        grad_proj,
        w_qkv_all.T,
        preferred_element_type=jnp.float32,
    )
    grad_tokens = (
        (cot_flat + grad_in).astype(jnp.bfloat16).reshape(LV, lat_rows, lon_cols, model_width)
    )
    tok_part = tok_flat
    att_part = attended
    partial = jnp.concatenate(
        [cross_rows(tok_part, grad_proj), cross_rows(att_part, grad_y)], axis=1
    ).astype(jnp.bfloat16)
    shard_sum = sum_rows(partial, "lon").astype(jnp.bfloat16)
    summed = sum_everywhere(shard_sum, "lat").astype(jnp.float32)
    grad_qkv = summed[:, : 3 * model_width]
    grad_out = summed[:, 3 * model_width :]
    return (output.reshape(LV, lat_rows, lon_cols, model_width), grad_tokens, grad_qkv, grad_out)


def solution(mesh):
    in_specs = (
        P(None, "lat", "lon", None),
        P("lon", None),
        P("lon", None),
        P(),
        P(),
        P(None, "lat", "lon", None),
    )
    out_specs = (
        P(None, "lat", "lon", None),
        P(None, "lat", "lon", None),
        P("lon", None),
        P("lon", None),
    )
    return jax.shard_map(
        on_device, mesh=mesh, in_specs=in_specs, out_specs=out_specs, check_vma=False
    )
```

```python
import jax
import jax.numpy as jnp
from jax import lax
from jax.sharding import PartitionSpec as P
from jax.experimental import pallas as pl
from jax.experimental.pallas import tpu as pltpu

LV = 4
WL = 2
WH = 6
WW = 12
KEYS = 288


NORM_EPS = 1e-05
UNIT_EPS = 1e-06
HEADS_K = 8
HD_K = 64


def _nt(a, b):
    return lax.dot_general(a, b, (((1,), (1,)), ((), ())), preferred_element_type=jnp.float32)


def _tn(a, b):
    return lax.dot_general(a, b, (((0,), (0,)), ((), ())), preferred_element_type=jnp.float32)


def _block_probs(tau_ref, head, query, kv_ref, mask_ref):
    lanes = pl.ds(head * HD_K, HD_K)
    weights = []
    for r in range(2):
        for c in range(2):
            scores = _nt(query, kv_ref[r, c, :, lanes]) * tau_ref[head]
            weights.append(jnp.exp(scores) * mask_ref[r])
    total = sum(jnp.sum(w, axis=-1, keepdims=True) for w in weights)
    return [w / total for w in weights]


def attn_fwd_kernel(tau_ref, q_ref, kv_ref, mask_ref, out_ref):
    width = q_ref.shape[3]
    for head in range(HEADS_K):
        lanes = pl.ds(head * HD_K, HD_K)
        value_lanes = pl.ds(width + head * HD_K, HD_K)
        probs = _block_probs(tau_ref, head, q_ref[0, 0, :, lanes], kv_ref, mask_ref)
        mixed = None
        for n, p in enumerate(probs):
            part = jnp.dot(
                p.astype(jnp.bfloat16),
                kv_ref[n // 2, n % 2, :, value_lanes],
                preferred_element_type=jnp.float32,
            )
            mixed = part if mixed is None else mixed + part
        out_ref[0, 0, :, lanes] = mixed


def attn_bwd_kernel(tau_ref, q_ref, kv_ref, g_ref, mask_ref, dq_ref, dkv_ref):
    width = q_ref.shape[3]
    for head in range(HEADS_K):
        lanes = pl.ds(head * HD_K, HD_K)
        value_lanes = pl.ds(width + head * HD_K, HD_K)
        query = q_ref[0, 0, :, lanes]
        grad = g_ref[0, 0, :, lanes]
        probs = _block_probs(tau_ref, head, query, kv_ref, mask_ref)
        dprobs = [_nt(grad, kv_ref[n // 2, n % 2, :, value_lanes]) for n in range(4)]
        total = sum(jnp.sum(p * d, axis=-1, keepdims=True) for p, d in zip(probs, dprobs))
        dquery = None
        for n in range(4):
            r, c = n // 2, n % 2
            dscore = (tau_ref[head] * (probs[n] * (dprobs[n] - total))).astype(jnp.bfloat16)
            part = jnp.dot(dscore, kv_ref[r, c, :, lanes], preferred_element_type=jnp.float32)
            dquery = part if dquery is None else dquery + part
            dkv_ref[r, c, :, lanes] = _tn(dscore, query)
            dkv_ref[r, c, :, value_lanes] = _tn(probs[n].astype(jnp.bfloat16), grad)
        dq_ref[0, 0, :, lanes] = dquery


def _window_of(i, j):
    return ((i + 1) // 2, (j + 1) // 2, 0, 0)


def window_fwd(tau, query, ext_kv, mask):
    row_units, col_units, queries, width = query.shape
    return pl.pallas_call(
        attn_fwd_kernel,
        grid=(row_units, col_units),
        in_specs=[
            pl.BlockSpec(memory_space=pltpu.SMEM),
            pl.BlockSpec((1, 1, queries, width), lambda i, j: (i, j, 0, 0)),
            pl.BlockSpec((2, 2, queries, 2 * width), _window_of),
            pl.BlockSpec((2, queries, queries), lambda i, j: ((i + 1) // 2, 0, 0)),
        ],
        out_specs=pl.BlockSpec((1, 1, queries, width), lambda i, j: (i, j, 0, 0)),
        out_shape=jax.ShapeDtypeStruct(query.shape, jnp.float32),
    )(tau, query, ext_kv, mask)


def window_bwd(tau, query, ext_kv, grad, mask):
    row_units, col_units, queries, width = query.shape
    return pl.pallas_call(
        attn_bwd_kernel,
        grid=(row_units, col_units),
        in_specs=[
            pl.BlockSpec(memory_space=pltpu.SMEM),
            pl.BlockSpec((1, 1, queries, width), lambda i, j: (i, j, 0, 0)),
            pl.BlockSpec((2, 2, queries, 2 * width), _window_of),
            pl.BlockSpec((1, 1, queries, width), lambda i, j: (i, j, 0, 0)),
            pl.BlockSpec((2, queries, queries), lambda i, j: ((i + 1) // 2, 0, 0)),
        ],
        out_specs=[
            pl.BlockSpec((1, 1, queries, width), lambda i, j: (i, j, 0, 0)),
            pl.BlockSpec((2, 2, queries, 2 * width), _window_of),
        ],
        out_shape=[
            jax.ShapeDtypeStruct(query.shape, jnp.float32),
            jax.ShapeDtypeStruct(ext_kv.shape, jnp.float32),
        ],
    )(tau, query, ext_kv, grad, mask)


def with_halo(shard, sides, width, wrap):
    for axis, dim in sides:
        peers, length = (lax.axis_size(axis), shard.shape[dim])
        up = [(i, (i + 1) % peers) for i in range(peers if wrap else peers - 1)]
        down = [(j, i) for i, j in up]
        last = lax.slice_in_dim(shard, length - width, length, axis=dim)
        initial = lax.slice_in_dim(shard, 0, width, axis=dim)
        before = lax.ppermute(last, axis, up)
        after = lax.ppermute(initial, axis, down)
        shard = jnp.concatenate([before, shard, after], axis=dim)
    return shard


def from_behind(block, axis, distance):
    devices = range(lax.axis_size(axis))
    route = [((i - distance) % len(devices), i) for i in devices]
    return lax.ppermute(block, axis, route)


def from_behind_2(block, axis, distance):
    devices = range(lax.axis_size(axis))
    route = [(i - distance, i) for i in devices if i - distance in devices]
    return lax.ppermute(block, axis, route)


def gather_rows(block, axis):
    peers = lax.axis_size(axis)
    copies = jnp.broadcast_to(block[None], (peers,) + block.shape)
    spread = lax.all_to_all(copies, axis, 0, 0, tiled=False)
    return spread.reshape((peers * block.shape[0],) + block.shape[1:])


def sum_rows(partial, axis):
    peers = lax.axis_size(axis)
    chunks = partial.reshape((peers, partial.shape[0] // peers) + partial.shape[1:])
    spread = lax.all_to_all(chunks, axis, 0, 0, tiled=False)
    return jnp.sum(spread.astype(jnp.float32), axis=0)


def sum_everywhere(partial, axis):
    peers = lax.axis_size(axis)
    own = sum_rows(partial, axis).astype(jnp.bfloat16)
    copies = jnp.broadcast_to(own[None], (peers,) + own.shape)
    spread = lax.all_to_all(copies, axis, 0, 0, tiled=False)
    return spread.reshape((peers * own.shape[0],) + own.shape[1:])


def unit_rows(vectors):
    scaling = lax.rsqrt(jnp.sum(vectors * vectors, axis=-1, keepdims=True) + UNIT_EPS)
    return (vectors * scaling, scaling)


def unit_back(vectors, scaling, gradient):
    inner_sum = jnp.sum(vectors * gradient, axis=-1, keepdims=True)
    return scaling * (gradient - vectors * (inner_sum * scaling * scaling))


def norm_forward(y_rows):
    centered = y_rows - jnp.mean(y_rows, axis=-1, keepdims=True)
    inverse = lax.rsqrt(jnp.mean(centered * centered, axis=-1, keepdims=True) + NORM_EPS)
    return (centered * inverse, inverse)


def norm_back(normed, inverse, upstream):
    mean_up = jnp.mean(upstream, axis=-1, keepdims=True)
    mean_cross = jnp.mean(upstream * normed, axis=-1, keepdims=True)
    return inverse * (upstream - mean_up - normed * mean_cross)


def query_units(own_grid):
    lat_rows = own_grid.shape[1]
    lon_cols = own_grid.shape[2]
    channels = own_grid.shape[3]
    half_h = WH // 2
    half_w = WW // 2
    shaped = own_grid.reshape(LV, lat_rows // half_h, half_h, lon_cols // half_w, half_w, channels)
    return shaped.transpose(1, 3, 0, 2, 4, 5).reshape(
        lat_rows // half_h, lon_cols // half_w, LV * half_h * half_w, channels
    )


def query_layout(units):
    row_units = units.shape[0]
    col_units = units.shape[1]
    channels = units.shape[3]
    half_h = WH // 2
    half_w = WW // 2
    shaped = units.reshape(row_units, col_units, LV, half_h, half_w, channels)
    return shaped.transpose(2, 0, 3, 1, 4, 5).reshape(
        LV, row_units * half_h, col_units * half_w, channels
    )


def cross_rows(left_mat, right_mat):
    return lax.dot_general(
        left_mat, right_mat, (((0,), (0,)), ((), ())), preferred_element_type=jnp.float32
    )


def on_device(tokens, w_qkv, w_out, gain, tau, cotangent):
    lat_rows = tokens.shape[1]
    model_width = tokens.shape[3]
    head_count = tau.shape[0]
    head_dim = model_width // head_count
    half_h = WH // 2
    half_w = WW // 2
    tok_units = query_units(tokens)
    row_units, col_units, query_count = tok_units.shape[:3]
    assert row_units == 2 and col_units == 2
    tok_count = row_units * col_units * query_count
    tok_flat = tok_units.reshape(tok_count, model_width)
    cot_flat = query_units(cotangent).reshape(tok_count, model_width).astype(jnp.float32)
    weights_all = gather_rows(jnp.concatenate([w_qkv, w_out], axis=1), "lon")
    w_qkv_all = weights_all[:, : 3 * model_width]
    w_out_all = weights_all[:, 3 * model_width :]
    projected = jnp.dot(tok_flat, w_qkv_all, preferred_element_type=jnp.float32)
    proj_b = projected.astype(jnp.bfloat16)
    query_f = proj_b[:, :model_width].astype(jnp.float32).reshape(tok_count, head_count, head_dim)
    key_f = (
        proj_b[:, model_width : 2 * model_width]
        .astype(jnp.float32)
        .reshape(tok_count, head_count, head_dim)
    )
    query_n, query_scale = unit_rows(query_f)
    key_n, key_scale = unit_rows(key_f)
    query_u = query_n.astype(jnp.bfloat16).reshape(row_units, col_units, query_count, model_width)
    key_b = key_n.astype(jnp.bfloat16).reshape(tok_count, model_width)
    kv_source = jnp.concatenate([key_b, proj_b[:, 2 * model_width :]], axis=1).reshape(
        row_units, col_units, query_count, 2 * model_width
    )
    ext_rows = with_halo(kv_source, (("lat", 0),), 1, False)
    ext_kv = with_halo(ext_rows, (("lon", 1),), 1, True)
    level_win = (jnp.arange(query_count) // (half_h * half_w) + WL // 2) // WL
    same_level = level_win[:, None] == level_win[None, :]
    block_row = jnp.arange(row_units + 2)
    first_row = lax.axis_index("lat") * lat_rows - half_h + half_h * block_row
    inside = (first_row >= 0) & (first_row < lat_rows * lax.axis_size("lat"))
    allowed = (same_level[None, :, :] & inside[:, None, None]).astype(jnp.float32)
    mixed = window_fwd(tau, query_u, ext_kv, allowed)
    attended = mixed.astype(jnp.bfloat16).reshape(tok_count, model_width)
    y_rows = jnp.dot(attended, w_out_all, preferred_element_type=jnp.float32)
    normed, inverse = norm_forward(y_rows)
    output = (tok_flat.astype(jnp.float32) + gain * normed).astype(jnp.bfloat16)
    grad_y = norm_back(normed, inverse, gain * cot_flat).astype(jnp.bfloat16)
    grad_att = jnp.dot(grad_y, w_out_all.T, preferred_element_type=jnp.float32)
    grad_u = grad_att.astype(jnp.bfloat16).reshape(row_units, col_units, query_count, model_width)
    dquery, ext_grad = window_bwd(tau, query_u, ext_kv, grad_u, allowed)
    grad_q = unit_back(
        query_f, query_scale, dquery.reshape(tok_count, head_count, head_dim)
    ).reshape(tok_count, model_width)
    west_rim = ext_grad[:, :1]
    east_rim = ext_grad[:, col_units + 1 :]
    center = ext_grad[:, 1 : col_units + 1]
    from_east = from_behind(west_rim.astype(jnp.bfloat16), "lon", -1).astype(west_rim.dtype)
    from_west = from_behind(east_rim.astype(jnp.bfloat16), "lon", 1).astype(east_rim.dtype)
    center = center.at[:, :1].add(from_west).at[:, col_units - 1 :].add(from_east)
    north_rim = center[:1]
    south_rim = center[row_units + 1 :]
    middle = center[1 : row_units + 1]
    from_south = from_behind_2(north_rim.astype(jnp.bfloat16), "lat", -1).astype(north_rim.dtype)
    from_north = from_behind_2(south_rim.astype(jnp.bfloat16), "lat", 1).astype(south_rim.dtype)
    middle = middle.at[:1].add(from_north).at[row_units - 1 :].add(from_south)
    own_grads = middle.reshape(tok_count, 2 * model_width)
    grad_k = unit_back(
        key_f, key_scale, own_grads[:, :model_width].reshape(tok_count, head_count, head_dim)
    ).reshape(tok_count, model_width)
    dvalue_src = own_grads[:, model_width:]
    grad_proj = jnp.concatenate([grad_q, grad_k, dvalue_src], axis=1).astype(jnp.bfloat16)
    grad_in = jnp.dot(grad_proj, w_qkv_all.T, preferred_element_type=jnp.float32)
    grad_tok = (cot_flat + grad_in).astype(jnp.bfloat16)
    partial = jnp.concatenate(
        [cross_rows(tok_flat, grad_proj), cross_rows(attended, grad_y)], axis=1
    ).astype(jnp.bfloat16)
    shard_sum = sum_rows(partial, "lon").astype(jnp.bfloat16)
    summed = sum_everywhere(shard_sum, "lat").astype(jnp.float32)
    grad_qkv = summed[:, : 3 * model_width]
    grad_out = summed[:, 3 * model_width :]
    unit_shape = (row_units, col_units, query_count, model_width)
    output = query_layout(output.reshape(unit_shape))
    grad_tokens = query_layout(grad_tok.reshape(unit_shape))
    return (output, grad_tokens, grad_qkv, grad_out)


def solution(mesh):
    in_specs = (
        P(None, "lat", "lon", None),
        P("lon", None),
        P("lon", None),
        P(),
        P(),
        P(None, "lat", "lon", None),
    )
    out_specs = (
        P(None, "lat", "lon", None),
        P(None, "lat", "lon", None),
        P("lon", None),
        P("lon", None),
    )
    return jax.shard_map(
        on_device, mesh=mesh, in_specs=in_specs, out_specs=out_specs, check_vma=False
    )
```

```python
import jax
import jax.numpy as jnp
from jax import lax
from jax.sharding import PartitionSpec as P
from jax.experimental import pallas as pl
from jax.experimental.pallas import tpu as pltpu

LV = 4
WL = 2
WH = 6
WW = 12
KEYS = 288


NORM_EPS = 1e-05
UNIT_EPS = 1e-06
HEADS_K = 8
HD_K = 64


def _nt(a, b):
    return lax.dot_general(a, b, (((1,), (1,)), ((), ())), preferred_element_type=jnp.float32)


def _tn(a, b):
    return lax.dot_general(a, b, (((0,), (0,)), ((), ())), preferred_element_type=jnp.float32)


def _block_probs(tau_ref, head, query, kv_ref, mask_ref):
    lanes = pl.ds(head * HD_K, HD_K)
    weights = []
    for r in range(2):
        for c in range(2):
            scores = _nt(query, kv_ref[r, c, :, lanes]) * tau_ref[head]
            weights.append(jnp.exp(scores) * mask_ref[r])
    total = sum(jnp.sum(w, axis=-1, keepdims=True) for w in weights)
    return [w / total for w in weights]


def attn_fwd_kernel(tau_ref, q_ref, kv_ref, mask_ref, out_ref):
    width = q_ref.shape[3]
    for head in range(HEADS_K):
        lanes = pl.ds(head * HD_K, HD_K)
        value_lanes = pl.ds(width + head * HD_K, HD_K)
        probs = _block_probs(tau_ref, head, q_ref[0, 0, :, lanes], kv_ref, mask_ref)
        mixed = None
        for n, p in enumerate(probs):
            part = jnp.dot(
                p.astype(jnp.bfloat16),
                kv_ref[n // 2, n % 2, :, value_lanes],
                preferred_element_type=jnp.float32,
            )
            mixed = part if mixed is None else mixed + part
        out_ref[0, 0, :, lanes] = mixed


def attn_bwd_kernel(tau_ref, q_ref, kv_ref, g_ref, mask_ref, dq_ref, dkv_ref):
    width = q_ref.shape[3]
    for head in range(HEADS_K):
        lanes = pl.ds(head * HD_K, HD_K)
        value_lanes = pl.ds(width + head * HD_K, HD_K)
        query = q_ref[0, 0, :, lanes]
        grad = g_ref[0, 0, :, lanes]
        probs = _block_probs(tau_ref, head, query, kv_ref, mask_ref)
        dprobs = [_nt(grad, kv_ref[n // 2, n % 2, :, value_lanes]) for n in range(4)]
        total = sum(jnp.sum(p * d, axis=-1, keepdims=True) for p, d in zip(probs, dprobs))
        dquery = None
        for n in range(4):
            r, c = n // 2, n % 2
            dscore = (tau_ref[head] * (probs[n] * (dprobs[n] - total))).astype(jnp.bfloat16)
            part = jnp.dot(dscore, kv_ref[r, c, :, lanes], preferred_element_type=jnp.float32)
            dquery = part if dquery is None else dquery + part
            dkv_ref[r, c, :, lanes] = _tn(dscore, query)
            dkv_ref[r, c, :, value_lanes] = _tn(probs[n].astype(jnp.bfloat16), grad)
        dq_ref[0, 0, :, lanes] = dquery


def _window_of(i, j):
    return ((i + 1) // 2, (j + 1) // 2, 0, 0)


def window_fwd(tau, query, ext_kv, mask):
    row_units, col_units, queries, width = query.shape
    return pl.pallas_call(
        attn_fwd_kernel,
        grid=(row_units, col_units),
        in_specs=[
            pl.BlockSpec(memory_space=pltpu.SMEM),
            pl.BlockSpec((1, 1, queries, width), lambda i, j: (i, j, 0, 0)),
            pl.BlockSpec((2, 2, queries, 2 * width), _window_of),
            pl.BlockSpec((2, queries, queries), lambda i, j: ((i + 1) // 2, 0, 0)),
        ],
        out_specs=pl.BlockSpec((1, 1, queries, width), lambda i, j: (i, j, 0, 0)),
        out_shape=jax.ShapeDtypeStruct(query.shape, jnp.float32),
    )(tau, query, ext_kv, mask)


def window_bwd(tau, query, ext_kv, grad, mask):
    row_units, col_units, queries, width = query.shape
    return pl.pallas_call(
        attn_bwd_kernel,
        grid=(row_units, col_units),
        in_specs=[
            pl.BlockSpec(memory_space=pltpu.SMEM),
            pl.BlockSpec((1, 1, queries, width), lambda i, j: (i, j, 0, 0)),
            pl.BlockSpec((2, 2, queries, 2 * width), _window_of),
            pl.BlockSpec((1, 1, queries, width), lambda i, j: (i, j, 0, 0)),
            pl.BlockSpec((2, queries, queries), lambda i, j: ((i + 1) // 2, 0, 0)),
        ],
        out_specs=[
            pl.BlockSpec((1, 1, queries, width), lambda i, j: (i, j, 0, 0)),
            pl.BlockSpec((2, 2, queries, 2 * width), _window_of),
        ],
        out_shape=[
            jax.ShapeDtypeStruct(query.shape, jnp.float32),
            jax.ShapeDtypeStruct(ext_kv.shape, jnp.float32),
        ],
    )(tau, query, ext_kv, grad, mask)


def with_halo(shard, sides, width, wrap):
    for axis, dim in sides:
        peers, length = (lax.axis_size(axis), shard.shape[dim])
        up = [(i, (i + 1) % peers) for i in range(peers if wrap else peers - 1)]
        down = [(j, i) for i, j in up]
        last = lax.slice_in_dim(shard, length - width, length, axis=dim)
        initial = lax.slice_in_dim(shard, 0, width, axis=dim)
        before = lax.ppermute(last, axis, up)
        after = lax.ppermute(initial, axis, down)
        shard = jnp.concatenate([before, shard, after], axis=dim)
    return shard


def from_behind(block, axis, distance):
    devices = range(lax.axis_size(axis))
    route = [((i - distance) % len(devices), i) for i in devices]
    return lax.ppermute(block, axis, route)


def from_behind_2(block, axis, distance):
    devices = range(lax.axis_size(axis))
    route = [(i - distance, i) for i in devices if i - distance in devices]
    return lax.ppermute(block, axis, route)


def gather_rows(block, axis):
    peers = lax.axis_size(axis)
    copies = jnp.broadcast_to(block[None], (peers,) + block.shape)
    spread = lax.all_to_all(copies, axis, 0, 0, tiled=False)
    return spread.reshape((peers * block.shape[0],) + block.shape[1:])


def sum_rows(partial, axis):
    peers = lax.axis_size(axis)
    chunks = partial.reshape((peers, partial.shape[0] // peers) + partial.shape[1:])
    spread = lax.all_to_all(chunks, axis, 0, 0, tiled=False)
    return jnp.sum(spread.astype(jnp.float32), axis=0)


def sum_everywhere(partial, axis):
    peers = lax.axis_size(axis)
    own = sum_rows(partial, axis).astype(jnp.bfloat16)
    copies = jnp.broadcast_to(own[None], (peers,) + own.shape)
    spread = lax.all_to_all(copies, axis, 0, 0, tiled=False)
    return spread.reshape((peers * own.shape[0],) + own.shape[1:])


def chip_partner(block):
    peers = lax.axis_size("lat")
    return lax.ppermute(block, "lat", [(i, i ^ 1) for i in range(peers)])


def gather_rows_paired(block, axis):
    core = lax.axis_index("lat") % 2
    halves = block.reshape(block.shape[0], 2, block.shape[1] // 2)
    mine = lax.dynamic_index_in_dim(halves, core, axis=1, keepdims=False)
    gathered = gather_rows(mine, axis)
    other = chip_partner(gathered)
    return jnp.where(
        core == 0,
        jnp.concatenate([gathered, other], axis=1),
        jnp.concatenate([other, gathered], axis=1),
    )


def sum_rows_paired(partial, axis):
    peers = lax.axis_size(axis)
    core = lax.axis_index("lat") % 2
    blocks = partial.reshape(peers, 2, partial.shape[0] // (2 * peers), partial.shape[1])
    keep = lax.dynamic_index_in_dim(blocks, core, axis=1, keepdims=False)
    give = lax.dynamic_index_in_dim(blocks, 1 - core, axis=1, keepdims=False)
    pair = keep.astype(jnp.float32) + chip_partner(give).astype(jnp.float32)
    own = sum_rows(pair.astype(jnp.bfloat16).reshape(-1, partial.shape[1]), axis)
    own = own.astype(jnp.bfloat16)
    empty = jnp.zeros_like(own)
    return jnp.where(
        core == 0,
        jnp.concatenate([own, empty], axis=0),
        jnp.concatenate([empty, own], axis=0),
    )


def unit_rows(vectors):
    scaling = lax.rsqrt(jnp.sum(vectors * vectors, axis=-1, keepdims=True) + UNIT_EPS)
    return (vectors * scaling, scaling)


def unit_back(vectors, scaling, gradient):
    inner_sum = jnp.sum(vectors * gradient, axis=-1, keepdims=True)
    return scaling * (gradient - vectors * (inner_sum * scaling * scaling))


def norm_forward(y_rows):
    centered = y_rows - jnp.mean(y_rows, axis=-1, keepdims=True)
    inverse = lax.rsqrt(jnp.mean(centered * centered, axis=-1, keepdims=True) + NORM_EPS)
    return (centered * inverse, inverse)


def norm_back(normed, inverse, upstream):
    mean_up = jnp.mean(upstream, axis=-1, keepdims=True)
    mean_cross = jnp.mean(upstream * normed, axis=-1, keepdims=True)
    return inverse * (upstream - mean_up - normed * mean_cross)


def query_units(own_grid):
    lat_rows = own_grid.shape[1]
    lon_cols = own_grid.shape[2]
    channels = own_grid.shape[3]
    half_h = WH // 2
    half_w = WW // 2
    shaped = own_grid.reshape(LV, lat_rows // half_h, half_h, lon_cols // half_w, half_w, channels)
    return shaped.transpose(1, 3, 0, 2, 4, 5).reshape(
        lat_rows // half_h, lon_cols // half_w, LV * half_h * half_w, channels
    )


def query_layout(units):
    row_units = units.shape[0]
    col_units = units.shape[1]
    channels = units.shape[3]
    half_h = WH // 2
    half_w = WW // 2
    shaped = units.reshape(row_units, col_units, LV, half_h, half_w, channels)
    return shaped.transpose(2, 0, 3, 1, 4, 5).reshape(
        LV, row_units * half_h, col_units * half_w, channels
    )


def cross_rows(left_mat, right_mat):
    return lax.dot_general(
        left_mat, right_mat, (((0,), (0,)), ((), ())), preferred_element_type=jnp.float32
    )


def on_device(tokens, w_qkv, w_out, gain, tau, cotangent):
    lat_rows = tokens.shape[1]
    model_width = tokens.shape[3]
    head_count = tau.shape[0]
    head_dim = model_width // head_count
    half_h = WH // 2
    half_w = WW // 2
    tok_units = query_units(tokens)
    row_units, col_units, query_count = tok_units.shape[:3]
    assert row_units == 2 and col_units == 2
    tok_count = row_units * col_units * query_count
    tok_flat = tok_units.reshape(tok_count, model_width)
    cot_flat = query_units(cotangent).reshape(tok_count, model_width).astype(jnp.float32)
    weights_all = gather_rows_paired(jnp.concatenate([w_qkv, w_out], axis=1), "lon")
    w_qkv_all = weights_all[:, : 3 * model_width]
    w_out_all = weights_all[:, 3 * model_width :]
    projected = jnp.dot(tok_flat, w_qkv_all, preferred_element_type=jnp.float32)
    proj_b = projected.astype(jnp.bfloat16)
    query_f = proj_b[:, :model_width].astype(jnp.float32).reshape(tok_count, head_count, head_dim)
    key_f = (
        proj_b[:, model_width : 2 * model_width]
        .astype(jnp.float32)
        .reshape(tok_count, head_count, head_dim)
    )
    query_n, query_scale = unit_rows(query_f)
    key_n, key_scale = unit_rows(key_f)
    query_u = query_n.astype(jnp.bfloat16).reshape(row_units, col_units, query_count, model_width)
    key_b = key_n.astype(jnp.bfloat16).reshape(tok_count, model_width)
    kv_source = jnp.concatenate([key_b, proj_b[:, 2 * model_width :]], axis=1).reshape(
        row_units, col_units, query_count, 2 * model_width
    )
    ext_rows = with_halo(kv_source, (("lat", 0),), 1, False)
    ext_kv = with_halo(ext_rows, (("lon", 1),), 1, True)
    level_win = (jnp.arange(query_count) // (half_h * half_w) + WL // 2) // WL
    same_level = level_win[:, None] == level_win[None, :]
    block_row = jnp.arange(row_units + 2)
    first_row = lax.axis_index("lat") * lat_rows - half_h + half_h * block_row
    inside = (first_row >= 0) & (first_row < lat_rows * lax.axis_size("lat"))
    allowed = (same_level[None, :, :] & inside[:, None, None]).astype(jnp.float32)
    mixed = window_fwd(tau, query_u, ext_kv, allowed)
    attended = mixed.astype(jnp.bfloat16).reshape(tok_count, model_width)
    y_rows = jnp.dot(attended, w_out_all, preferred_element_type=jnp.float32)
    normed, inverse = norm_forward(y_rows)
    output = (tok_flat.astype(jnp.float32) + gain * normed).astype(jnp.bfloat16)
    grad_y = norm_back(normed, inverse, gain * cot_flat).astype(jnp.bfloat16)
    grad_att = jnp.dot(grad_y, w_out_all.T, preferred_element_type=jnp.float32)
    grad_u = grad_att.astype(jnp.bfloat16).reshape(row_units, col_units, query_count, model_width)
    dquery, ext_grad = window_bwd(tau, query_u, ext_kv, grad_u, allowed)
    grad_q = unit_back(
        query_f, query_scale, dquery.reshape(tok_count, head_count, head_dim)
    ).reshape(tok_count, model_width)
    west_rim = ext_grad[:, :1]
    east_rim = ext_grad[:, col_units + 1 :]
    center = ext_grad[:, 1 : col_units + 1]
    from_east = from_behind(west_rim.astype(jnp.bfloat16), "lon", -1).astype(west_rim.dtype)
    from_west = from_behind(east_rim.astype(jnp.bfloat16), "lon", 1).astype(east_rim.dtype)
    center = center.at[:, :1].add(from_west).at[:, col_units - 1 :].add(from_east)
    north_rim = center[:1]
    south_rim = center[row_units + 1 :]
    middle = center[1 : row_units + 1]
    from_south = from_behind_2(north_rim.astype(jnp.bfloat16), "lat", -1).astype(north_rim.dtype)
    from_north = from_behind_2(south_rim.astype(jnp.bfloat16), "lat", 1).astype(south_rim.dtype)
    middle = middle.at[:1].add(from_north).at[row_units - 1 :].add(from_south)
    own_grads = middle.reshape(tok_count, 2 * model_width)
    grad_k = unit_back(
        key_f, key_scale, own_grads[:, :model_width].reshape(tok_count, head_count, head_dim)
    ).reshape(tok_count, model_width)
    dvalue_src = own_grads[:, model_width:]
    grad_proj = jnp.concatenate([grad_q, grad_k, dvalue_src], axis=1).astype(jnp.bfloat16)
    grad_in = jnp.dot(grad_proj, w_qkv_all.T, preferred_element_type=jnp.float32)
    grad_tok = (cot_flat + grad_in).astype(jnp.bfloat16)
    partial = jnp.concatenate(
        [cross_rows(tok_flat, grad_proj), cross_rows(attended, grad_y)], axis=1
    ).astype(jnp.bfloat16)
    shard_sum = sum_rows_paired(partial, "lon")
    summed = sum_everywhere(shard_sum, "lat").astype(jnp.float32)
    grad_qkv = summed[:, : 3 * model_width]
    grad_out = summed[:, 3 * model_width :]
    unit_shape = (row_units, col_units, query_count, model_width)
    output = query_layout(output.reshape(unit_shape))
    grad_tokens = query_layout(grad_tok.reshape(unit_shape))
    return (output, grad_tokens, grad_qkv, grad_out)


def solution(mesh):
    in_specs = (
        P(None, "lat", "lon", None),
        P("lon", None),
        P("lon", None),
        P(),
        P(),
        P(None, "lat", "lon", None),
    )
    out_specs = (
        P(None, "lat", "lon", None),
        P(None, "lat", "lon", None),
        P("lon", None),
        P("lon", None),
    )
    return jax.shard_map(
        on_device, mesh=mesh, in_specs=in_specs, out_specs=out_specs, check_vma=False
    )
```

```python
import jax
import jax.numpy as jnp
from jax import lax
from jax.sharding import PartitionSpec as P
from jax.experimental import pallas as pl
from jax.experimental.pallas import tpu as pltpu

LV = 4
WL = 2
WH = 6
WW = 12
KEYS = 288


NORM_EPS = 1e-05
UNIT_EPS = 1e-06
HEADS_K = 8
HD_K = 64


def _nt(a, b):
    return lax.dot_general(a, b, (((1,), (1,)), ((), ())), preferred_element_type=jnp.float32)


def _tn(a, b):
    return lax.dot_general(a, b, (((0,), (0,)), ((), ())), preferred_element_type=jnp.float32)


def _block_probs(tau_ref, head, query, kv_ref, mask_ref):
    lanes = pl.ds(head * HD_K, HD_K)
    weights = []
    for r in range(2):
        for c in range(2):
            scores = _nt(query, kv_ref[r, c, :, lanes]) * tau_ref[head]
            weights.append(jnp.exp(scores) * mask_ref[r])
    total = sum(jnp.sum(w, axis=-1, keepdims=True) for w in weights)
    return [w / total for w in weights]


def attn_fwd_kernel(tau_ref, q_ref, kv_ref, mask_ref, out_ref):
    width = q_ref.shape[3]
    for head in range(HEADS_K):
        lanes = pl.ds(head * HD_K, HD_K)
        value_lanes = pl.ds(width + head * HD_K, HD_K)
        probs = _block_probs(tau_ref, head, q_ref[0, 0, :, lanes], kv_ref, mask_ref)
        mixed = None
        for n, p in enumerate(probs):
            part = jnp.dot(
                p.astype(jnp.bfloat16),
                kv_ref[n // 2, n % 2, :, value_lanes],
                preferred_element_type=jnp.float32,
            )
            mixed = part if mixed is None else mixed + part
        out_ref[0, 0, :, lanes] = mixed


def attn_bwd_kernel(tau_ref, q_ref, kv_ref, g_ref, mask_ref, dq_ref, dkv_ref):
    width = q_ref.shape[3]
    for head in range(HEADS_K):
        lanes = pl.ds(head * HD_K, HD_K)
        value_lanes = pl.ds(width + head * HD_K, HD_K)
        query = q_ref[0, 0, :, lanes]
        grad = g_ref[0, 0, :, lanes]
        probs = _block_probs(tau_ref, head, query, kv_ref, mask_ref)
        dprobs = [_nt(grad, kv_ref[n // 2, n % 2, :, value_lanes]) for n in range(4)]
        total = sum(jnp.sum(p * d, axis=-1, keepdims=True) for p, d in zip(probs, dprobs))
        dquery = None
        for n in range(4):
            r, c = n // 2, n % 2
            dscore = (tau_ref[head] * (probs[n] * (dprobs[n] - total))).astype(jnp.bfloat16)
            part = jnp.dot(dscore, kv_ref[r, c, :, lanes], preferred_element_type=jnp.float32)
            dquery = part if dquery is None else dquery + part
            dkv_ref[r, c, :, lanes] = _tn(dscore, query)
            dkv_ref[r, c, :, value_lanes] = _tn(probs[n].astype(jnp.bfloat16), grad)
        dq_ref[0, 0, :, lanes] = dquery


def _window_of(i, j):
    return ((i + 1) // 2, (j + 1) // 2, 0, 0)


def window_fwd(tau, query, ext_kv, mask):
    row_units, col_units, queries, width = query.shape
    return pl.pallas_call(
        attn_fwd_kernel,
        grid=(row_units, col_units),
        in_specs=[
            pl.BlockSpec(memory_space=pltpu.SMEM),
            pl.BlockSpec((1, 1, queries, width), lambda i, j: (i, j, 0, 0)),
            pl.BlockSpec((2, 2, queries, 2 * width), _window_of),
            pl.BlockSpec((2, queries, queries), lambda i, j: ((i + 1) // 2, 0, 0)),
        ],
        out_specs=pl.BlockSpec((1, 1, queries, width), lambda i, j: (i, j, 0, 0)),
        out_shape=jax.ShapeDtypeStruct(query.shape, jnp.float32),
    )(tau, query, ext_kv, mask)


def window_bwd(tau, query, ext_kv, grad, mask):
    row_units, col_units, queries, width = query.shape
    return pl.pallas_call(
        attn_bwd_kernel,
        grid=(row_units, col_units),
        in_specs=[
            pl.BlockSpec(memory_space=pltpu.SMEM),
            pl.BlockSpec((1, 1, queries, width), lambda i, j: (i, j, 0, 0)),
            pl.BlockSpec((2, 2, queries, 2 * width), _window_of),
            pl.BlockSpec((1, 1, queries, width), lambda i, j: (i, j, 0, 0)),
            pl.BlockSpec((2, queries, queries), lambda i, j: ((i + 1) // 2, 0, 0)),
        ],
        out_specs=[
            pl.BlockSpec((1, 1, queries, width), lambda i, j: (i, j, 0, 0)),
            pl.BlockSpec((2, 2, queries, 2 * width), _window_of),
        ],
        out_shape=[
            jax.ShapeDtypeStruct(query.shape, jnp.float32),
            jax.ShapeDtypeStruct(ext_kv.shape, jnp.float32),
        ],
    )(tau, query, ext_kv, grad, mask)


def gather_rows(block, axis):
    peers = lax.axis_size(axis)
    copies = jnp.broadcast_to(block[None], (peers,) + block.shape)
    spread = lax.all_to_all(copies, axis, 0, 0, tiled=False)
    return spread.reshape((peers * block.shape[0],) + block.shape[1:])


def sum_rows(partial, axis):
    peers = lax.axis_size(axis)
    chunks = partial.reshape((peers, partial.shape[0] // peers) + partial.shape[1:])
    spread = lax.all_to_all(chunks, axis, 0, 0, tiled=False)
    return jnp.sum(spread.astype(jnp.float32), axis=0)


def sum_everywhere(partial, axis):
    peers = lax.axis_size(axis)
    own = sum_rows(partial, axis).astype(jnp.bfloat16)
    copies = jnp.broadcast_to(own[None], (peers,) + own.shape)
    spread = lax.all_to_all(copies, axis, 0, 0, tiled=False)
    return spread.reshape((peers * own.shape[0],) + own.shape[1:])


def shift_grid(block, down, right):
    rows, cols = lax.axis_size("lat"), lax.axis_size("lon")
    if down == 0:
        return lax.ppermute(block, "lon", [(j, (j + right) % cols) for j in range(cols)])
    pairs = [
        (i * cols + j, (i + down) * cols + (j + right) % cols)
        for i in range(rows)
        if 0 <= i + down < rows
        for j in range(cols)
    ]
    if right == 0:
        return lax.ppermute(block, "lat", [(i, i + down) for i in range(rows) if 0 <= i + down < rows])
    return lax.ppermute(block, ("lat", "lon"), pairs)


def with_ring(units):
    up = shift_grid(units[1], 1, 0)
    down = shift_grid(units[0], -1, 0)
    left = shift_grid(units[:, 1], 0, 1)
    right = shift_grid(units[:, 0], 0, -1)
    top = [shift_grid(units[1, 1], 1, 1), up[0], up[1], shift_grid(units[1, 0], 1, -1)]
    bottom = [shift_grid(units[0, 1], -1, 1), down[0], down[1], shift_grid(units[0, 0], -1, -1)]
    middle = [[left[r], units[r, 0], units[r, 1], right[r]] for r in range(2)]
    return jnp.stack([jnp.stack(row) for row in [top] + middle + [bottom]])


def fold_ring(ext):
    def back(block, down, right):
        return shift_grid(block.astype(jnp.bfloat16), down, right).astype(ext.dtype)

    own = ext[1:3, 1:3]
    own = own.at[0].add(back(ext[3, 1:3], 1, 0)).at[1].add(back(ext[0, 1:3], -1, 0))
    own = own.at[:, 0].add(back(ext[1:3, 3], 0, 1)).at[:, 1].add(back(ext[1:3, 0], 0, -1))
    own = own.at[0, 0].add(back(ext[3, 3], 1, 1)).at[0, 1].add(back(ext[3, 0], 1, -1))
    return own.at[1, 0].add(back(ext[0, 3], -1, 1)).at[1, 1].add(back(ext[0, 0], -1, -1))


def chip_partner(block):
    peers = lax.axis_size("lat")
    return lax.ppermute(block, "lat", [(i, i ^ 1) for i in range(peers)])


def gather_rows_paired(block, axis):
    core = lax.axis_index("lat") % 2
    halves = block.reshape(block.shape[0], 2, block.shape[1] // 2)
    mine = lax.dynamic_index_in_dim(halves, core, axis=1, keepdims=False)
    gathered = gather_rows(mine, axis)
    other = chip_partner(gathered)
    return jnp.where(
        core == 0,
        jnp.concatenate([gathered, other], axis=1),
        jnp.concatenate([other, gathered], axis=1),
    )


def sum_rows_paired(partial, axis):
    peers = lax.axis_size(axis)
    core = lax.axis_index("lat") % 2
    blocks = partial.reshape(peers, 2, partial.shape[0] // (2 * peers), partial.shape[1])
    keep = lax.dynamic_index_in_dim(blocks, core, axis=1, keepdims=False)
    give = lax.dynamic_index_in_dim(blocks, 1 - core, axis=1, keepdims=False)
    pair = keep.astype(jnp.float32) + chip_partner(give).astype(jnp.float32)
    own = sum_rows(pair.astype(jnp.bfloat16).reshape(-1, partial.shape[1]), axis)
    own = own.astype(jnp.bfloat16)
    empty = jnp.zeros_like(own)
    return jnp.where(
        core == 0,
        jnp.concatenate([own, empty], axis=0),
        jnp.concatenate([empty, own], axis=0),
    )


def unit_rows(vectors):
    scaling = lax.rsqrt(jnp.sum(vectors * vectors, axis=-1, keepdims=True) + UNIT_EPS)
    return (vectors * scaling, scaling)


def unit_back(vectors, scaling, gradient):
    inner_sum = jnp.sum(vectors * gradient, axis=-1, keepdims=True)
    return scaling * (gradient - vectors * (inner_sum * scaling * scaling))


def norm_forward(y_rows):
    centered = y_rows - jnp.mean(y_rows, axis=-1, keepdims=True)
    inverse = lax.rsqrt(jnp.mean(centered * centered, axis=-1, keepdims=True) + NORM_EPS)
    return (centered * inverse, inverse)


def norm_back(normed, inverse, upstream):
    mean_up = jnp.mean(upstream, axis=-1, keepdims=True)
    mean_cross = jnp.mean(upstream * normed, axis=-1, keepdims=True)
    return inverse * (upstream - mean_up - normed * mean_cross)


def query_units(own_grid):
    lat_rows = own_grid.shape[1]
    lon_cols = own_grid.shape[2]
    channels = own_grid.shape[3]
    half_h = WH // 2
    half_w = WW // 2
    shaped = own_grid.reshape(LV, lat_rows // half_h, half_h, lon_cols // half_w, half_w, channels)
    return shaped.transpose(1, 3, 0, 2, 4, 5).reshape(
        lat_rows // half_h, lon_cols // half_w, LV * half_h * half_w, channels
    )


def query_layout(units):
    row_units = units.shape[0]
    col_units = units.shape[1]
    channels = units.shape[3]
    half_h = WH // 2
    half_w = WW // 2
    shaped = units.reshape(row_units, col_units, LV, half_h, half_w, channels)
    return shaped.transpose(2, 0, 3, 1, 4, 5).reshape(
        LV, row_units * half_h, col_units * half_w, channels
    )


def cross_rows(left_mat, right_mat):
    return lax.dot_general(
        left_mat, right_mat, (((0,), (0,)), ((), ())), preferred_element_type=jnp.float32
    )


def on_device(tokens, w_qkv, w_out, gain, tau, cotangent):
    lat_rows = tokens.shape[1]
    model_width = tokens.shape[3]
    head_count = tau.shape[0]
    head_dim = model_width // head_count
    half_h = WH // 2
    half_w = WW // 2
    tok_units = query_units(tokens)
    row_units, col_units, query_count = tok_units.shape[:3]
    assert row_units == 2 and col_units == 2
    tok_count = row_units * col_units * query_count
    tok_flat = tok_units.reshape(tok_count, model_width)
    cot_flat = query_units(cotangent).reshape(tok_count, model_width).astype(jnp.float32)
    weights_all = gather_rows_paired(jnp.concatenate([w_qkv, w_out], axis=1), "lon")
    w_qkv_all = weights_all[:, : 3 * model_width]
    w_out_all = weights_all[:, 3 * model_width :]
    projected = jnp.dot(tok_flat, w_qkv_all, preferred_element_type=jnp.float32)
    proj_b = projected.astype(jnp.bfloat16)
    query_f = proj_b[:, :model_width].astype(jnp.float32).reshape(tok_count, head_count, head_dim)
    key_f = (
        proj_b[:, model_width : 2 * model_width]
        .astype(jnp.float32)
        .reshape(tok_count, head_count, head_dim)
    )
    query_n, query_scale = unit_rows(query_f)
    key_n, key_scale = unit_rows(key_f)
    query_u = query_n.astype(jnp.bfloat16).reshape(row_units, col_units, query_count, model_width)
    key_b = key_n.astype(jnp.bfloat16).reshape(tok_count, model_width)
    kv_source = jnp.concatenate([key_b, proj_b[:, 2 * model_width :]], axis=1).reshape(
        row_units, col_units, query_count, 2 * model_width
    )
    ext_kv = with_ring(kv_source)
    level_win = (jnp.arange(query_count) // (half_h * half_w) + WL // 2) // WL
    same_level = level_win[:, None] == level_win[None, :]
    block_row = jnp.arange(row_units + 2)
    first_row = lax.axis_index("lat") * lat_rows - half_h + half_h * block_row
    inside = (first_row >= 0) & (first_row < lat_rows * lax.axis_size("lat"))
    allowed = (same_level[None, :, :] & inside[:, None, None]).astype(jnp.float32)
    mixed = window_fwd(tau, query_u, ext_kv, allowed)
    attended = mixed.astype(jnp.bfloat16).reshape(tok_count, model_width)
    y_rows = jnp.dot(attended, w_out_all, preferred_element_type=jnp.float32)
    normed, inverse = norm_forward(y_rows)
    output = (tok_flat.astype(jnp.float32) + gain * normed).astype(jnp.bfloat16)
    grad_y = norm_back(normed, inverse, gain * cot_flat).astype(jnp.bfloat16)
    grad_att = jnp.dot(grad_y, w_out_all.T, preferred_element_type=jnp.float32)
    grad_u = grad_att.astype(jnp.bfloat16).reshape(row_units, col_units, query_count, model_width)
    dquery, ext_grad = window_bwd(tau, query_u, ext_kv, grad_u, allowed)
    grad_q = unit_back(
        query_f, query_scale, dquery.reshape(tok_count, head_count, head_dim)
    ).reshape(tok_count, model_width)
    middle = fold_ring(ext_grad)
    own_grads = middle.reshape(tok_count, 2 * model_width)
    grad_k = unit_back(
        key_f, key_scale, own_grads[:, :model_width].reshape(tok_count, head_count, head_dim)
    ).reshape(tok_count, model_width)
    dvalue_src = own_grads[:, model_width:]
    grad_proj = jnp.concatenate([grad_q, grad_k, dvalue_src], axis=1).astype(jnp.bfloat16)
    grad_in = jnp.dot(grad_proj, w_qkv_all.T, preferred_element_type=jnp.float32)
    grad_tok = (cot_flat + grad_in).astype(jnp.bfloat16)
    partial = jnp.concatenate(
        [cross_rows(tok_flat, grad_proj), cross_rows(attended, grad_y)], axis=1
    ).astype(jnp.bfloat16)
    shard_sum = sum_rows_paired(partial, "lon")
    summed = sum_everywhere(shard_sum, "lat").astype(jnp.float32)
    grad_qkv = summed[:, : 3 * model_width]
    grad_out = summed[:, 3 * model_width :]
    unit_shape = (row_units, col_units, query_count, model_width)
    output = query_layout(output.reshape(unit_shape))
    grad_tokens = query_layout(grad_tok.reshape(unit_shape))
    return (output, grad_tokens, grad_qkv, grad_out)


def solution(mesh):
    in_specs = (
        P(None, "lat", "lon", None),
        P("lon", None),
        P("lon", None),
        P(),
        P(),
        P(None, "lat", "lon", None),
    )
    out_specs = (
        P(None, "lat", "lon", None),
        P(None, "lat", "lon", None),
        P("lon", None),
        P("lon", None),
    )
    return jax.shard_map(
        on_device, mesh=mesh, in_specs=in_specs, out_specs=out_specs, check_vma=False
    )
```

```python
import jax
import jax.numpy as jnp
from jax import lax
from jax.sharding import PartitionSpec as P
from jax.experimental import pallas as pl
from jax.experimental.pallas import tpu as pltpu

LV = 4
WL = 2
WH = 6
WW = 12
KEYS = 288


NORM_EPS = 1e-05
UNIT_EPS = 1e-06
HEADS_K = 8
HD_K = 64


def _nt(a, b):
    return lax.dot_general(a, b, (((1,), (1,)), ((), ())), preferred_element_type=jnp.float32)


def _tn(a, b):
    return lax.dot_general(a, b, (((0,), (0,)), ((), ())), preferred_element_type=jnp.float32)


def _window_probs(tau_ref, head, query, keys, mask):
    scores = _nt(query, keys) * tau_ref[head]
    weights = jnp.exp(scores) * mask
    return weights / jnp.sum(weights, axis=-1, keepdims=True)


def _head_keys(kv_ref, lanes):
    rows, cols, block = kv_ref.shape[:3]
    return kv_ref[:, :, :, lanes].reshape(rows * cols * block, HD_K)


def attn_fwd_kernel(tau_ref, q_ref, kv_ref, mask_ref, out_ref):
    width = q_ref.shape[3]
    mask = mask_ref[0]
    for head in range(HEADS_K):
        lanes = pl.ds(head * HD_K, HD_K)
        value_lanes = pl.ds(width + head * HD_K, HD_K)
        probs = _window_probs(tau_ref, head, q_ref[0, 0, :, lanes], _head_keys(kv_ref, lanes), mask)
        out_ref[0, 0, :, lanes] = jnp.dot(
            probs.astype(jnp.bfloat16),
            _head_keys(kv_ref, value_lanes),
            preferred_element_type=jnp.float32,
        )


def attn_bwd_kernel(tau_ref, q_ref, kv_ref, g_ref, mask_ref, dq_ref, dkv_ref):
    width = q_ref.shape[3]
    mask = mask_ref[0]
    for head in range(HEADS_K):
        lanes = pl.ds(head * HD_K, HD_K)
        value_lanes = pl.ds(width + head * HD_K, HD_K)
        query = q_ref[0, 0, :, lanes]
        grad = g_ref[0, 0, :, lanes]
        keys = _head_keys(kv_ref, lanes)
        probs = _window_probs(tau_ref, head, query, keys, mask)
        dprob = _nt(grad, _head_keys(kv_ref, value_lanes))
        total = jnp.sum(probs * dprob, axis=-1, keepdims=True)
        dscore = (tau_ref[head] * (probs * (dprob - total))).astype(jnp.bfloat16)
        dq_ref[0, 0, :, lanes] = jnp.dot(dscore, keys, preferred_element_type=jnp.float32)
        dkv_ref[:, :, :, lanes] = _tn(dscore, query).reshape(dkv_ref.shape[:3] + (HD_K,))
        dkv_ref[:, :, :, value_lanes] = _tn(probs.astype(jnp.bfloat16), grad).reshape(
            dkv_ref.shape[:3] + (HD_K,)
        )


def _window_of(i, j):
    return ((i + 1) // 2, (j + 1) // 2, 0, 0)


def window_fwd(tau, query, ext_kv, mask):
    row_units, col_units, queries, width = query.shape
    block = ext_kv.shape[2]
    return pl.pallas_call(
        attn_fwd_kernel,
        grid=(row_units, col_units),
        in_specs=[
            pl.BlockSpec(memory_space=pltpu.SMEM),
            pl.BlockSpec((1, 1, queries, width), lambda i, j: (i, j, 0, 0)),
            pl.BlockSpec((2, 2, block, 2 * width), _window_of),
            pl.BlockSpec((1, queries, mask.shape[2]), lambda i, j: ((i + 1) // 2, 0, 0)),
        ],
        out_specs=pl.BlockSpec((1, 1, queries, width), lambda i, j: (i, j, 0, 0)),
        out_shape=jax.ShapeDtypeStruct(query.shape, jnp.float32),
    )(tau, query, ext_kv, mask)


def window_bwd(tau, query, ext_kv, grad, mask):
    row_units, col_units, queries, width = query.shape
    block = ext_kv.shape[2]
    return pl.pallas_call(
        attn_bwd_kernel,
        grid=(row_units, col_units),
        in_specs=[
            pl.BlockSpec(memory_space=pltpu.SMEM),
            pl.BlockSpec((1, 1, queries, width), lambda i, j: (i, j, 0, 0)),
            pl.BlockSpec((2, 2, block, 2 * width), _window_of),
            pl.BlockSpec((1, 1, queries, width), lambda i, j: (i, j, 0, 0)),
            pl.BlockSpec((1, queries, mask.shape[2]), lambda i, j: ((i + 1) // 2, 0, 0)),
        ],
        out_specs=[
            pl.BlockSpec((1, 1, queries, width), lambda i, j: (i, j, 0, 0)),
            pl.BlockSpec((2, 2, block, 2 * width), _window_of),
        ],
        out_shape=[
            jax.ShapeDtypeStruct(query.shape, jnp.float32),
            jax.ShapeDtypeStruct(ext_kv.shape, jnp.float32),
        ],
    )(tau, query, ext_kv, grad, mask)


def with_halo(shard, sides, width, wrap):
    for axis, dim in sides:
        peers, length = (lax.axis_size(axis), shard.shape[dim])
        up = [(i, (i + 1) % peers) for i in range(peers if wrap else peers - 1)]
        down = [(j, i) for i, j in up]
        last = lax.slice_in_dim(shard, length - width, length, axis=dim)
        initial = lax.slice_in_dim(shard, 0, width, axis=dim)
        before = lax.ppermute(last, axis, up)
        after = lax.ppermute(initial, axis, down)
        shard = jnp.concatenate([before, shard, after], axis=dim)
    return shard


def from_behind(block, axis, distance):
    devices = range(lax.axis_size(axis))
    route = [((i - distance) % len(devices), i) for i in devices]
    return lax.ppermute(block, axis, route)


def from_behind_2(block, axis, distance):
    devices = range(lax.axis_size(axis))
    route = [(i - distance, i) for i in devices if i - distance in devices]
    return lax.ppermute(block, axis, route)


def gather_rows(block, axis):
    peers = lax.axis_size(axis)
    copies = jnp.broadcast_to(block[None], (peers,) + block.shape)
    spread = lax.all_to_all(copies, axis, 0, 0, tiled=False)
    return spread.reshape((peers * block.shape[0],) + block.shape[1:])


def sum_rows(partial, axis):
    peers = lax.axis_size(axis)
    chunks = partial.reshape((peers, partial.shape[0] // peers) + partial.shape[1:])
    spread = lax.all_to_all(chunks, axis, 0, 0, tiled=False)
    return jnp.sum(spread.astype(jnp.float32), axis=0)


def sum_everywhere(partial, axis):
    peers = lax.axis_size(axis)
    own = sum_rows(partial, axis).astype(jnp.bfloat16)
    copies = jnp.broadcast_to(own[None], (peers,) + own.shape)
    spread = lax.all_to_all(copies, axis, 0, 0, tiled=False)
    return spread.reshape((peers * own.shape[0],) + own.shape[1:])


def chip_partner(block):
    peers = lax.axis_size("lat")
    return lax.ppermute(block, "lat", [(i, i ^ 1) for i in range(peers)])


def gather_rows_paired(block, axis):
    core = lax.axis_index("lat") % 2
    halves = block.reshape(block.shape[0], 2, block.shape[1] // 2)
    mine = lax.dynamic_index_in_dim(halves, core, axis=1, keepdims=False)
    gathered = gather_rows(mine, axis)
    other = chip_partner(gathered)
    return jnp.where(
        core == 0,
        jnp.concatenate([gathered, other], axis=1),
        jnp.concatenate([other, gathered], axis=1),
    )


def sum_rows_paired(partial, axis):
    peers = lax.axis_size(axis)
    core = lax.axis_index("lat") % 2
    blocks = partial.reshape(peers, 2, partial.shape[0] // (2 * peers), partial.shape[1])
    keep = lax.dynamic_index_in_dim(blocks, core, axis=1, keepdims=False)
    give = lax.dynamic_index_in_dim(blocks, 1 - core, axis=1, keepdims=False)
    pair = keep.astype(jnp.float32) + chip_partner(give).astype(jnp.float32)
    own = sum_rows(pair.astype(jnp.bfloat16).reshape(-1, partial.shape[1]), axis)
    own = own.astype(jnp.bfloat16)
    empty = jnp.zeros_like(own)
    return jnp.where(
        core == 0,
        jnp.concatenate([own, empty], axis=0),
        jnp.concatenate([empty, own], axis=0),
    )


def unit_rows(vectors):
    scaling = lax.rsqrt(jnp.sum(vectors * vectors, axis=-1, keepdims=True) + UNIT_EPS)
    return (vectors * scaling, scaling)


def unit_back(vectors, scaling, gradient):
    inner_sum = jnp.sum(vectors * gradient, axis=-1, keepdims=True)
    return scaling * (gradient - vectors * (inner_sum * scaling * scaling))


def norm_forward(y_rows):
    centered = y_rows - jnp.mean(y_rows, axis=-1, keepdims=True)
    inverse = lax.rsqrt(jnp.mean(centered * centered, axis=-1, keepdims=True) + NORM_EPS)
    return (centered * inverse, inverse)


def norm_back(normed, inverse, upstream):
    mean_up = jnp.mean(upstream, axis=-1, keepdims=True)
    mean_cross = jnp.mean(upstream * normed, axis=-1, keepdims=True)
    return inverse * (upstream - mean_up - normed * mean_cross)


def query_units(own_grid):
    lat_rows = own_grid.shape[1]
    lon_cols = own_grid.shape[2]
    channels = own_grid.shape[3]
    half_h = WH // 2
    half_w = WW // 2
    shaped = own_grid.reshape(LV, lat_rows // half_h, half_h, lon_cols // half_w, half_w, channels)
    return shaped.transpose(1, 3, 0, 2, 4, 5).reshape(
        lat_rows // half_h, lon_cols // half_w, LV * half_h * half_w, channels
    )


def query_layout(units):
    row_units = units.shape[0]
    col_units = units.shape[1]
    channels = units.shape[3]
    half_h = WH // 2
    half_w = WW // 2
    shaped = units.reshape(row_units, col_units, LV, half_h, half_w, channels)
    return shaped.transpose(2, 0, 3, 1, 4, 5).reshape(
        LV, row_units * half_h, col_units * half_w, channels
    )


def cross_rows(left_mat, right_mat):
    return lax.dot_general(
        left_mat, right_mat, (((0,), (0,)), ((), ())), preferred_element_type=jnp.float32
    )


def on_device(tokens, w_qkv, w_out, gain, tau, cotangent):
    lat_rows = tokens.shape[1]
    model_width = tokens.shape[3]
    head_count = tau.shape[0]
    head_dim = model_width // head_count
    half_h = WH // 2
    half_w = WW // 2
    tok_units = query_units(tokens)
    row_units, col_units, query_count = tok_units.shape[:3]
    assert row_units == 2 and col_units == 2
    tok_count = row_units * col_units * query_count
    tok_flat = tok_units.reshape(tok_count, model_width)
    cot_flat = query_units(cotangent).reshape(tok_count, model_width).astype(jnp.float32)
    weights_all = gather_rows_paired(jnp.concatenate([w_qkv, w_out], axis=1), "lon")
    w_qkv_all = weights_all[:, : 3 * model_width]
    w_out_all = weights_all[:, 3 * model_width :]
    projected = jnp.dot(tok_flat, w_qkv_all, preferred_element_type=jnp.float32)
    proj_b = projected.astype(jnp.bfloat16)
    query_f = proj_b[:, :model_width].astype(jnp.float32).reshape(tok_count, head_count, head_dim)
    key_f = (
        proj_b[:, model_width : 2 * model_width]
        .astype(jnp.float32)
        .reshape(tok_count, head_count, head_dim)
    )
    query_n, query_scale = unit_rows(query_f)
    key_n, key_scale = unit_rows(key_f)
    query_u = query_n.astype(jnp.bfloat16).reshape(row_units, col_units, query_count, model_width)
    key_b = key_n.astype(jnp.bfloat16).reshape(tok_count, model_width)
    kv_source = jnp.concatenate([key_b, proj_b[:, 2 * model_width :]], axis=1).reshape(
        row_units, col_units, query_count, 2 * model_width
    )
    ext_rows = with_halo(kv_source, (("lat", 0),), 1, False)
    ext_kv = with_halo(ext_rows, (("lon", 1),), 1, True)
    block = 16 * pl.cdiv(query_count, 16)
    ext_kv = jnp.pad(ext_kv, ((0, 0), (0, 0), (0, block - query_count), (0, 0)))
    level_win = (jnp.arange(block) // (half_h * half_w) + WL // 2) // WL
    same_level = (level_win[:query_count, None] == level_win[None, :]) & (
        jnp.arange(block) < query_count
    )
    block_row = jnp.arange(row_units + 2)
    first_row = lax.axis_index("lat") * lat_rows - half_h + half_h * block_row
    inside = (first_row >= 0) & (first_row < lat_rows * lax.axis_size("lat"))
    allowed = same_level[None, :, :] & inside[:, None, None]
    allowed = allowed.reshape(-1, 2, 1, query_count, block)
    allowed = jnp.broadcast_to(allowed, allowed.shape[:2] + (2, query_count, block))
    allowed = allowed.transpose(0, 3, 1, 2, 4).reshape(-1, query_count, 4 * block)
    allowed = allowed.astype(jnp.float32)
    mixed = window_fwd(tau, query_u, ext_kv, allowed)
    attended = mixed.astype(jnp.bfloat16).reshape(tok_count, model_width)
    y_rows = jnp.dot(attended, w_out_all, preferred_element_type=jnp.float32)
    normed, inverse = norm_forward(y_rows)
    output = (tok_flat.astype(jnp.float32) + gain * normed).astype(jnp.bfloat16)
    grad_y = norm_back(normed, inverse, gain * cot_flat).astype(jnp.bfloat16)
    grad_att = jnp.dot(grad_y, w_out_all.T, preferred_element_type=jnp.float32)
    grad_u = grad_att.astype(jnp.bfloat16).reshape(row_units, col_units, query_count, model_width)
    dquery, ext_grad = window_bwd(tau, query_u, ext_kv, grad_u, allowed)
    ext_grad = ext_grad[:, :, :query_count]
    grad_q = unit_back(
        query_f, query_scale, dquery.reshape(tok_count, head_count, head_dim)
    ).reshape(tok_count, model_width)
    west_rim = ext_grad[:, :1]
    east_rim = ext_grad[:, col_units + 1 :]
    center = ext_grad[:, 1 : col_units + 1]
    from_east = from_behind(west_rim.astype(jnp.bfloat16), "lon", -1).astype(west_rim.dtype)
    from_west = from_behind(east_rim.astype(jnp.bfloat16), "lon", 1).astype(east_rim.dtype)
    center = center.at[:, :1].add(from_west).at[:, col_units - 1 :].add(from_east)
    north_rim = center[:1]
    south_rim = center[row_units + 1 :]
    middle = center[1 : row_units + 1]
    from_south = from_behind_2(north_rim.astype(jnp.bfloat16), "lat", -1).astype(north_rim.dtype)
    from_north = from_behind_2(south_rim.astype(jnp.bfloat16), "lat", 1).astype(south_rim.dtype)
    middle = middle.at[:1].add(from_north).at[row_units - 1 :].add(from_south)
    own_grads = middle.reshape(tok_count, 2 * model_width)
    grad_k = unit_back(
        key_f, key_scale, own_grads[:, :model_width].reshape(tok_count, head_count, head_dim)
    ).reshape(tok_count, model_width)
    dvalue_src = own_grads[:, model_width:]
    grad_proj = jnp.concatenate([grad_q, grad_k, dvalue_src], axis=1).astype(jnp.bfloat16)
    grad_in = jnp.dot(grad_proj, w_qkv_all.T, preferred_element_type=jnp.float32)
    grad_tok = (cot_flat + grad_in).astype(jnp.bfloat16)
    partial = jnp.concatenate(
        [cross_rows(tok_flat, grad_proj), cross_rows(attended, grad_y)], axis=1
    ).astype(jnp.bfloat16)
    shard_sum = sum_rows_paired(partial, "lon")
    summed = sum_everywhere(shard_sum, "lat").astype(jnp.float32)
    grad_qkv = summed[:, : 3 * model_width]
    grad_out = summed[:, 3 * model_width :]
    unit_shape = (row_units, col_units, query_count, model_width)
    output = query_layout(output.reshape(unit_shape))
    grad_tokens = query_layout(grad_tok.reshape(unit_shape))
    return (output, grad_tokens, grad_qkv, grad_out)


def solution(mesh):
    in_specs = (
        P(None, "lat", "lon", None),
        P("lon", None),
        P("lon", None),
        P(),
        P(),
        P(None, "lat", "lon", None),
    )
    out_specs = (
        P(None, "lat", "lon", None),
        P(None, "lat", "lon", None),
        P("lon", None),
        P("lon", None),
    )
    return jax.shard_map(
        on_device, mesh=mesh, in_specs=in_specs, out_specs=out_specs, check_vma=False
    )
```

```python
import jax
import jax.numpy as jnp
from jax import lax
from jax.sharding import PartitionSpec as P
from jax.experimental import pallas as pl
from jax.experimental.pallas import tpu as pltpu

LV = 4
WL = 2
WH = 6
WW = 12
KEYS = 288


NORM_EPS = 1e-05
UNIT_EPS = 1e-06
HEADS_K = 8
HD_K = 64


def _nt(a, b):
    return lax.dot_general(a, b, (((1,), (1,)), ((), ())), preferred_element_type=jnp.float32)


def _tn(a, b):
    return lax.dot_general(a, b, (((0,), (0,)), ((), ())), preferred_element_type=jnp.float32)


def _window_probs(tau_ref, head, query, keys, mask):
    scores = _nt(query, keys) * tau_ref[head]
    weights = jnp.exp(scores) * mask
    return weights / jnp.sum(weights, axis=-1, keepdims=True)


def _head_keys(kv_ref, lanes):
    rows, cols, block = kv_ref.shape[:3]
    return kv_ref[:, :, :, lanes].reshape(rows * cols * block, HD_K)


def attn_fwd_kernel(tau_ref, q_ref, kv_ref, mask_ref, out_ref):
    width = q_ref.shape[3]
    mask = mask_ref[0]
    for head in range(HEADS_K):
        lanes = pl.ds(head * HD_K, HD_K)
        value_lanes = pl.ds(width + head * HD_K, HD_K)
        probs = _window_probs(tau_ref, head, q_ref[0, 0, :, lanes], _head_keys(kv_ref, lanes), mask)
        out_ref[0, 0, :, lanes] = jnp.dot(
            probs.astype(jnp.bfloat16),
            _head_keys(kv_ref, value_lanes),
            preferred_element_type=jnp.float32,
        )


def attn_bwd_kernel(tau_ref, q_ref, kv_ref, g_ref, mask_ref, dq_ref, dkv_ref):
    width = q_ref.shape[3]
    mask = mask_ref[0]
    for head in range(HEADS_K):
        lanes = pl.ds(head * HD_K, HD_K)
        value_lanes = pl.ds(width + head * HD_K, HD_K)
        query = q_ref[0, 0, :, lanes]
        grad = g_ref[0, 0, :, lanes]
        keys = _head_keys(kv_ref, lanes)
        probs = _window_probs(tau_ref, head, query, keys, mask)
        dprob = _nt(grad, _head_keys(kv_ref, value_lanes))
        total = jnp.sum(probs * dprob, axis=-1, keepdims=True)
        dscore = (tau_ref[head] * (probs * (dprob - total))).astype(jnp.bfloat16)
        dq_ref[0, 0, :, lanes] = jnp.dot(dscore, keys, preferred_element_type=jnp.float32)
        dkv_ref[:, :, :, lanes] = _tn(dscore, query).reshape(dkv_ref.shape[:3] + (HD_K,))
        dkv_ref[:, :, :, value_lanes] = _tn(probs.astype(jnp.bfloat16), grad).reshape(
            dkv_ref.shape[:3] + (HD_K,)
        )


def _window_of(i, j):
    return ((i + 1) // 2, (j + 1) // 2, 0, 0)


def window_fwd(tau, query, ext_kv, mask):
    row_units, col_units, queries, width = query.shape
    block = ext_kv.shape[2]
    return pl.pallas_call(
        attn_fwd_kernel,
        grid=(row_units, col_units),
        in_specs=[
            pl.BlockSpec(memory_space=pltpu.SMEM),
            pl.BlockSpec((1, 1, queries, width), lambda i, j: (i, j, 0, 0)),
            pl.BlockSpec((2, 2, block, 2 * width), _window_of),
            pl.BlockSpec((1, queries, mask.shape[2]), lambda i, j: ((i + 1) // 2, 0, 0)),
        ],
        out_specs=pl.BlockSpec((1, 1, queries, width), lambda i, j: (i, j, 0, 0)),
        out_shape=jax.ShapeDtypeStruct(query.shape, jnp.float32),
    )(tau, query, ext_kv, mask)


def window_bwd(tau, query, ext_kv, grad, mask):
    row_units, col_units, queries, width = query.shape
    block = ext_kv.shape[2]
    return pl.pallas_call(
        attn_bwd_kernel,
        grid=(row_units, col_units),
        in_specs=[
            pl.BlockSpec(memory_space=pltpu.SMEM),
            pl.BlockSpec((1, 1, queries, width), lambda i, j: (i, j, 0, 0)),
            pl.BlockSpec((2, 2, block, 2 * width), _window_of),
            pl.BlockSpec((1, 1, queries, width), lambda i, j: (i, j, 0, 0)),
            pl.BlockSpec((1, queries, mask.shape[2]), lambda i, j: ((i + 1) // 2, 0, 0)),
        ],
        out_specs=[
            pl.BlockSpec((1, 1, queries, width), lambda i, j: (i, j, 0, 0)),
            pl.BlockSpec((2, 2, block, 2 * width), _window_of),
        ],
        out_shape=[
            jax.ShapeDtypeStruct(query.shape, jnp.float32),
            jax.ShapeDtypeStruct(ext_kv.shape, jnp.float32),
        ],
    )(tau, query, ext_kv, grad, mask)


def with_halo(shard, sides, width, wrap):
    for axis, dim in sides:
        peers, length = (lax.axis_size(axis), shard.shape[dim])
        up = [(i, (i + 1) % peers) for i in range(peers if wrap else peers - 1)]
        down = [(j, i) for i, j in up]
        last = lax.slice_in_dim(shard, length - width, length, axis=dim)
        initial = lax.slice_in_dim(shard, 0, width, axis=dim)
        before = lax.ppermute(last, axis, up)
        after = lax.ppermute(initial, axis, down)
        shard = jnp.concatenate([before, shard, after], axis=dim)
    return shard


def from_behind(block, axis, distance):
    devices = range(lax.axis_size(axis))
    route = [((i - distance) % len(devices), i) for i in devices]
    return lax.ppermute(block, axis, route)


def from_behind_2(block, axis, distance):
    devices = range(lax.axis_size(axis))
    route = [(i - distance, i) for i in devices if i - distance in devices]
    return lax.ppermute(block, axis, route)


def gather_rows(block, axis):
    peers = lax.axis_size(axis)
    copies = jnp.broadcast_to(block[None], (peers,) + block.shape)
    spread = lax.all_to_all(copies, axis, 0, 0, tiled=False)
    return spread.reshape((peers * block.shape[0],) + block.shape[1:])


def sum_rows(partial, axis):
    peers = lax.axis_size(axis)
    chunks = partial.reshape((peers, partial.shape[0] // peers) + partial.shape[1:])
    spread = lax.all_to_all(chunks, axis, 0, 0, tiled=False)
    return jnp.sum(spread.astype(jnp.float32), axis=0)


def sum_everywhere(partial, axis):
    peers = lax.axis_size(axis)
    own = sum_rows(partial, axis).astype(jnp.bfloat16)
    copies = jnp.broadcast_to(own[None], (peers,) + own.shape)
    spread = lax.all_to_all(copies, axis, 0, 0, tiled=False)
    return spread.reshape((peers * own.shape[0],) + own.shape[1:])


def chip_partner(block):
    peers = lax.axis_size("lat")
    return lax.ppermute(block, "lat", [(i, i ^ 1) for i in range(peers)])


def gather_rows_paired(block, axis):
    core = lax.axis_index("lat") % 2
    halves = block.reshape(block.shape[0], 2, block.shape[1] // 2)
    mine = lax.dynamic_index_in_dim(halves, core, axis=1, keepdims=False)
    gathered = gather_rows(mine, axis)
    other = chip_partner(gathered)
    return jnp.where(
        core == 0,
        jnp.concatenate([gathered, other], axis=1),
        jnp.concatenate([other, gathered], axis=1),
    )


def sum_rows_paired(partial, axis):
    peers = lax.axis_size(axis)
    core = lax.axis_index("lat") % 2
    blocks = partial.reshape(peers, 2, partial.shape[0] // (2 * peers), partial.shape[1])
    keep = lax.dynamic_index_in_dim(blocks, core, axis=1, keepdims=False)
    give = lax.dynamic_index_in_dim(blocks, 1 - core, axis=1, keepdims=False)
    pair = keep.astype(jnp.float32) + chip_partner(give).astype(jnp.float32)
    own = sum_rows(pair.astype(jnp.bfloat16).reshape(-1, partial.shape[1]), axis)
    own = own.astype(jnp.bfloat16)
    empty = jnp.zeros_like(own)
    return jnp.where(
        core == 0,
        jnp.concatenate([own, empty], axis=0),
        jnp.concatenate([empty, own], axis=0),
    )


def unit_rows(vectors):
    scaling = lax.rsqrt(jnp.sum(vectors * vectors, axis=-1, keepdims=True) + UNIT_EPS)
    return (vectors * scaling, scaling)


def unit_back(vectors, scaling, gradient):
    inner_sum = jnp.sum(vectors * gradient, axis=-1, keepdims=True)
    return scaling * (gradient - vectors * (inner_sum * scaling * scaling))


def norm_forward(y_rows):
    centered = y_rows - jnp.mean(y_rows, axis=-1, keepdims=True)
    inverse = lax.rsqrt(jnp.mean(centered * centered, axis=-1, keepdims=True) + NORM_EPS)
    return (centered * inverse, inverse)


def norm_back(normed, inverse, upstream):
    mean_up = jnp.mean(upstream, axis=-1, keepdims=True)
    mean_cross = jnp.mean(upstream * normed, axis=-1, keepdims=True)
    return inverse * (upstream - mean_up - normed * mean_cross)


def query_units(own_grid):
    lat_rows = own_grid.shape[1]
    lon_cols = own_grid.shape[2]
    channels = own_grid.shape[3]
    half_h = WH // 2
    half_w = WW // 2
    shaped = own_grid.reshape(LV, lat_rows // half_h, half_h, lon_cols // half_w, half_w, channels)
    return shaped.transpose(1, 3, 0, 2, 4, 5).reshape(
        lat_rows // half_h, lon_cols // half_w, LV * half_h * half_w, channels
    )


def query_layout(units):
    row_units = units.shape[0]
    col_units = units.shape[1]
    channels = units.shape[3]
    half_h = WH // 2
    half_w = WW // 2
    shaped = units.reshape(row_units, col_units, LV, half_h, half_w, channels)
    return shaped.transpose(2, 0, 3, 1, 4, 5).reshape(
        LV, row_units * half_h, col_units * half_w, channels
    )


def cross_rows(left_mat, right_mat):
    return lax.dot_general(
        left_mat, right_mat, (((0,), (0,)), ((), ())), preferred_element_type=jnp.float32
    )


def on_device(tokens, w_qkv, w_out, gain, tau, cotangent):
    lat_rows = tokens.shape[1]
    model_width = tokens.shape[3]
    head_count = tau.shape[0]
    head_dim = model_width // head_count
    half_h = WH // 2
    half_w = WW // 2
    tok_units = query_units(tokens)
    row_units, col_units, query_count = tok_units.shape[:3]
    assert row_units == 2 and col_units == 2
    tok_count = row_units * col_units * query_count
    tok_flat = tok_units.reshape(tok_count, model_width)
    cot_flat = query_units(cotangent).reshape(tok_count, model_width).astype(jnp.float32)
    weights_all = gather_rows_paired(jnp.concatenate([w_qkv, w_out], axis=1), "lon")
    w_qkv_all = weights_all[:, : 3 * model_width]
    w_out_all = weights_all[:, 3 * model_width :]
    projected = jnp.dot(tok_flat, w_qkv_all, preferred_element_type=jnp.float32)
    proj_b = projected.astype(jnp.bfloat16)
    query_f = proj_b[:, :model_width].astype(jnp.float32).reshape(tok_count, head_count, head_dim)
    key_f = (
        proj_b[:, model_width : 2 * model_width]
        .astype(jnp.float32)
        .reshape(tok_count, head_count, head_dim)
    )
    query_n, query_scale = unit_rows(query_f)
    key_n, key_scale = unit_rows(key_f)
    query_u = query_n.astype(jnp.bfloat16).reshape(row_units, col_units, query_count, model_width)
    key_b = key_n.astype(jnp.bfloat16).reshape(tok_count, model_width)
    kv_source = jnp.concatenate([key_b, proj_b[:, 2 * model_width :]], axis=1).reshape(
        row_units, col_units, query_count, 2 * model_width
    )
    ext_cols = with_halo(kv_source, (("lon", 1),), 1, True)
    ext_kv = with_halo(ext_cols, (("lat", 0),), 1, False)
    block = 16 * pl.cdiv(query_count, 16)
    ext_kv = jnp.pad(ext_kv, ((0, 0), (0, 0), (0, block - query_count), (0, 0)))
    level_win = (jnp.arange(block) // (half_h * half_w) + WL // 2) // WL
    same_level = (level_win[:query_count, None] == level_win[None, :]) & (
        jnp.arange(block) < query_count
    )
    block_row = jnp.arange(row_units + 2)
    first_row = lax.axis_index("lat") * lat_rows - half_h + half_h * block_row
    inside = (first_row >= 0) & (first_row < lat_rows * lax.axis_size("lat"))
    allowed = same_level[None, :, :] & inside[:, None, None]
    allowed = allowed.reshape(-1, 2, 1, query_count, block)
    allowed = jnp.broadcast_to(allowed, allowed.shape[:2] + (2, query_count, block))
    allowed = allowed.transpose(0, 3, 1, 2, 4).reshape(-1, query_count, 4 * block)
    allowed = allowed.astype(jnp.float32)
    mixed = window_fwd(tau, query_u, ext_kv, allowed)
    attended = mixed.astype(jnp.bfloat16).reshape(tok_count, model_width)
    y_rows = jnp.dot(attended, w_out_all, preferred_element_type=jnp.float32)
    normed, inverse = norm_forward(y_rows)
    output = (tok_flat.astype(jnp.float32) + gain * normed).astype(jnp.bfloat16)
    grad_y = norm_back(normed, inverse, gain * cot_flat).astype(jnp.bfloat16)
    grad_att = jnp.dot(grad_y, w_out_all.T, preferred_element_type=jnp.float32)
    grad_u = grad_att.astype(jnp.bfloat16).reshape(row_units, col_units, query_count, model_width)
    dquery, ext_grad = window_bwd(tau, query_u, ext_kv, grad_u, allowed)
    ext_grad = ext_grad[:, :, :query_count]
    grad_q = unit_back(
        query_f, query_scale, dquery.reshape(tok_count, head_count, head_dim)
    ).reshape(tok_count, model_width)
    north_rim = ext_grad[:1]
    south_rim = ext_grad[row_units + 1 :]
    rows = ext_grad[1 : row_units + 1]
    from_south = from_behind_2(north_rim.astype(jnp.bfloat16), "lat", -1).astype(north_rim.dtype)
    from_north = from_behind_2(south_rim.astype(jnp.bfloat16), "lat", 1).astype(south_rim.dtype)
    rows = rows.at[:1].add(from_north).at[row_units - 1 :].add(from_south)
    west_rim = rows[:, :1]
    east_rim = rows[:, col_units + 1 :]
    middle = rows[:, 1 : col_units + 1]
    from_east = from_behind(west_rim.astype(jnp.bfloat16), "lon", -1).astype(west_rim.dtype)
    from_west = from_behind(east_rim.astype(jnp.bfloat16), "lon", 1).astype(east_rim.dtype)
    middle = middle.at[:, :1].add(from_west).at[:, col_units - 1 :].add(from_east)
    own_grads = middle.reshape(tok_count, 2 * model_width)
    grad_k = unit_back(
        key_f, key_scale, own_grads[:, :model_width].reshape(tok_count, head_count, head_dim)
    ).reshape(tok_count, model_width)
    dvalue_src = own_grads[:, model_width:]
    grad_proj = jnp.concatenate([grad_q, grad_k, dvalue_src], axis=1).astype(jnp.bfloat16)
    grad_in = jnp.dot(grad_proj, w_qkv_all.T, preferred_element_type=jnp.float32)
    grad_tok = (cot_flat + grad_in).astype(jnp.bfloat16)
    partial = jnp.concatenate(
        [cross_rows(tok_flat, grad_proj), cross_rows(attended, grad_y)], axis=1
    ).astype(jnp.bfloat16)
    shard_sum = sum_rows_paired(partial, "lon")
    summed = sum_everywhere(shard_sum, "lat").astype(jnp.float32)
    grad_qkv = summed[:, : 3 * model_width]
    grad_out = summed[:, 3 * model_width :]
    unit_shape = (row_units, col_units, query_count, model_width)
    output = query_layout(output.reshape(unit_shape))
    grad_tokens = query_layout(grad_tok.reshape(unit_shape))
    return (output, grad_tokens, grad_qkv, grad_out)


def solution(mesh):
    in_specs = (
        P(None, "lat", "lon", None),
        P("lon", None),
        P("lon", None),
        P(),
        P(),
        P(None, "lat", "lon", None),
    )
    out_specs = (
        P(None, "lat", "lon", None),
        P(None, "lat", "lon", None),
        P("lon", None),
        P("lon", None),
    )
    return jax.shard_map(
        on_device, mesh=mesh, in_specs=in_specs, out_specs=out_specs, check_vma=False
    )
```

```python
import jax
import jax.numpy as jnp
from jax import lax
from jax.sharding import PartitionSpec as P
from jax.experimental import pallas as pl
from jax.experimental.pallas import tpu as pltpu

LV = 4
WL = 2
WH = 6
WW = 12
KEYS = 288


NORM_EPS = 1e-05
UNIT_EPS = 1e-06
HEADS_K = 8
HD_K = 64


def _nt(a, b):
    return lax.dot_general(a, b, (((1,), (1,)), ((), ())), preferred_element_type=jnp.float32)


def _tn(a, b):
    return lax.dot_general(a, b, (((0,), (0,)), ((), ())), preferred_element_type=jnp.float32)


def _window_probs(tau, query, keys, mask):
    scores = _nt(query, keys) * tau
    weights = jnp.exp(scores) * mask
    return weights / jnp.sum(weights, axis=-1, keepdims=True)


def _pair_lanes(pair, width=0):
    return pl.ds(width + 2 * pair * HD_K, 2 * HD_K)


def _pair_keys(kv_ref, lanes):
    rows, cols, block = kv_ref.shape[:3]
    return kv_ref[:, :, :, lanes].reshape(rows * cols * block, 2 * HD_K)


def _split_pair(block, low):
    zero = jnp.zeros_like(block)
    return jnp.where(low, block, zero), jnp.where(low, zero, block)


def attn_fwd_kernel(tau_ref, q_ref, kv_ref, mask_ref, out_ref):
    width = q_ref.shape[3]
    mask = mask_ref[0]
    for pair in range(HEADS_K // 2):
        lanes, value_lanes = _pair_lanes(pair), _pair_lanes(pair, width)
        query = q_ref[0, 0, :, lanes]
        low = lax.broadcasted_iota(jnp.int32, query.shape, 1) < HD_K
        keys = _pair_keys(kv_ref, lanes)
        values = _pair_keys(kv_ref, value_lanes)
        mixed = []
        for half, part in enumerate(_split_pair(query, low)):
            probs = _window_probs(tau_ref[2 * pair + half], part, keys, mask)
            mixed.append(
                jnp.dot(probs.astype(jnp.bfloat16), values, preferred_element_type=jnp.float32)
            )
        out_ref[0, 0, :, lanes] = jnp.where(low, mixed[0], mixed[1])


def attn_bwd_kernel(tau_ref, q_ref, kv_ref, g_ref, mask_ref, dq_ref, dkv_ref):
    width = q_ref.shape[3]
    mask = mask_ref[0]
    for pair in range(HEADS_K // 2):
        lanes, value_lanes = _pair_lanes(pair), _pair_lanes(pair, width)
        query = q_ref[0, 0, :, lanes]
        grad = g_ref[0, 0, :, lanes]
        low = lax.broadcasted_iota(jnp.int32, query.shape, 1) < HD_K
        keys = _pair_keys(kv_ref, lanes)
        values = _pair_keys(kv_ref, value_lanes)
        queries = _split_pair(query, low)
        grads = _split_pair(grad, low)
        dq, dk, dv = [], [], []
        for half in range(2):
            tau = tau_ref[2 * pair + half]
            probs = _window_probs(tau, queries[half], keys, mask)
            dprob = _nt(grads[half], values)
            total = jnp.sum(probs * dprob, axis=-1, keepdims=True)
            dscore = (tau * (probs * (dprob - total))).astype(jnp.bfloat16)
            dq.append(jnp.dot(dscore, keys, preferred_element_type=jnp.float32))
            dk.append(_tn(dscore, query))
            dv.append(_tn(probs.astype(jnp.bfloat16), grad))
        dq_ref[0, 0, :, lanes] = jnp.where(low, dq[0], dq[1])
        key_low = lax.broadcasted_iota(jnp.int32, keys.shape, 1) < HD_K
        out_shape = dkv_ref.shape[:3] + (2 * HD_K,)
        dkv_ref[:, :, :, lanes] = jnp.where(key_low, dk[0], dk[1]).reshape(out_shape)
        dkv_ref[:, :, :, value_lanes] = jnp.where(key_low, dv[0], dv[1]).reshape(out_shape)


def _window_of(i, j):
    return ((i + 1) // 2, (j + 1) // 2, 0, 0)


def window_fwd(tau, query, ext_kv, mask):
    row_units, col_units, queries, width = query.shape
    block = ext_kv.shape[2]
    return pl.pallas_call(
        attn_fwd_kernel,
        grid=(row_units, col_units),
        in_specs=[
            pl.BlockSpec(memory_space=pltpu.SMEM),
            pl.BlockSpec((1, 1, queries, width), lambda i, j: (i, j, 0, 0)),
            pl.BlockSpec((2, 2, block, 2 * width), _window_of),
            pl.BlockSpec((1, queries, mask.shape[2]), lambda i, j: ((i + 1) // 2, 0, 0)),
        ],
        out_specs=pl.BlockSpec((1, 1, queries, width), lambda i, j: (i, j, 0, 0)),
        out_shape=jax.ShapeDtypeStruct(query.shape, jnp.float32),
    )(tau, query, ext_kv, mask)


def window_bwd(tau, query, ext_kv, grad, mask):
    row_units, col_units, queries, width = query.shape
    block = ext_kv.shape[2]
    return pl.pallas_call(
        attn_bwd_kernel,
        grid=(row_units, col_units),
        in_specs=[
            pl.BlockSpec(memory_space=pltpu.SMEM),
            pl.BlockSpec((1, 1, queries, width), lambda i, j: (i, j, 0, 0)),
            pl.BlockSpec((2, 2, block, 2 * width), _window_of),
            pl.BlockSpec((1, 1, queries, width), lambda i, j: (i, j, 0, 0)),
            pl.BlockSpec((1, queries, mask.shape[2]), lambda i, j: ((i + 1) // 2, 0, 0)),
        ],
        out_specs=[
            pl.BlockSpec((1, 1, queries, width), lambda i, j: (i, j, 0, 0)),
            pl.BlockSpec((2, 2, block, 2 * width), _window_of),
        ],
        out_shape=[
            jax.ShapeDtypeStruct(query.shape, jnp.float32),
            jax.ShapeDtypeStruct(ext_kv.shape, jnp.float32),
        ],
    )(tau, query, ext_kv, grad, mask)


def with_halo(shard, sides, width, wrap):
    for axis, dim in sides:
        peers, length = (lax.axis_size(axis), shard.shape[dim])
        up = [(i, (i + 1) % peers) for i in range(peers if wrap else peers - 1)]
        down = [(j, i) for i, j in up]
        last = lax.slice_in_dim(shard, length - width, length, axis=dim)
        initial = lax.slice_in_dim(shard, 0, width, axis=dim)
        before = lax.ppermute(last, axis, up)
        after = lax.ppermute(initial, axis, down)
        shard = jnp.concatenate([before, shard, after], axis=dim)
    return shard


def from_behind(block, axis, distance):
    devices = range(lax.axis_size(axis))
    route = [((i - distance) % len(devices), i) for i in devices]
    return lax.ppermute(block, axis, route)


def from_behind_2(block, axis, distance):
    devices = range(lax.axis_size(axis))
    route = [(i - distance, i) for i in devices if i - distance in devices]
    return lax.ppermute(block, axis, route)


def gather_rows(block, axis):
    peers = lax.axis_size(axis)
    copies = jnp.broadcast_to(block[None], (peers,) + block.shape)
    spread = lax.all_to_all(copies, axis, 0, 0, tiled=False)
    return spread.reshape((peers * block.shape[0],) + block.shape[1:])


def sum_rows(partial, axis):
    peers = lax.axis_size(axis)
    chunks = partial.reshape((peers, partial.shape[0] // peers) + partial.shape[1:])
    spread = lax.all_to_all(chunks, axis, 0, 0, tiled=False)
    return jnp.sum(spread.astype(jnp.float32), axis=0)


def sum_everywhere(partial, axis):
    peers = lax.axis_size(axis)
    own = sum_rows(partial, axis).astype(jnp.bfloat16)
    copies = jnp.broadcast_to(own[None], (peers,) + own.shape)
    spread = lax.all_to_all(copies, axis, 0, 0, tiled=False)
    return spread.reshape((peers * own.shape[0],) + own.shape[1:])


def chip_partner(block):
    peers = lax.axis_size("lat")
    return lax.ppermute(block, "lat", [(i, i ^ 1) for i in range(peers)])


def gather_rows_paired(block, axis):
    core = lax.axis_index("lat") % 2
    halves = block.reshape(block.shape[0], 2, block.shape[1] // 2)
    mine = lax.dynamic_index_in_dim(halves, core, axis=1, keepdims=False)
    gathered = gather_rows(mine, axis)
    other = chip_partner(gathered)
    return jnp.where(
        core == 0,
        jnp.concatenate([gathered, other], axis=1),
        jnp.concatenate([other, gathered], axis=1),
    )


def sum_rows_paired(partial, axis):
    peers = lax.axis_size(axis)
    core = lax.axis_index("lat") % 2
    blocks = partial.reshape(peers, 2, partial.shape[0] // (2 * peers), partial.shape[1])
    keep = lax.dynamic_index_in_dim(blocks, core, axis=1, keepdims=False)
    give = lax.dynamic_index_in_dim(blocks, 1 - core, axis=1, keepdims=False)
    pair = keep.astype(jnp.float32) + chip_partner(give).astype(jnp.float32)
    own = sum_rows(pair.astype(jnp.bfloat16).reshape(-1, partial.shape[1]), axis)
    own = own.astype(jnp.bfloat16)
    empty = jnp.zeros_like(own)
    return jnp.where(
        core == 0,
        jnp.concatenate([own, empty], axis=0),
        jnp.concatenate([empty, own], axis=0),
    )


def unit_rows(vectors):
    scaling = lax.rsqrt(jnp.sum(vectors * vectors, axis=-1, keepdims=True) + UNIT_EPS)
    return (vectors * scaling, scaling)


def unit_back(vectors, scaling, gradient):
    inner_sum = jnp.sum(vectors * gradient, axis=-1, keepdims=True)
    return scaling * (gradient - vectors * (inner_sum * scaling * scaling))


def norm_forward(y_rows):
    centered = y_rows - jnp.mean(y_rows, axis=-1, keepdims=True)
    inverse = lax.rsqrt(jnp.mean(centered * centered, axis=-1, keepdims=True) + NORM_EPS)
    return (centered * inverse, inverse)


def norm_back(normed, inverse, upstream):
    mean_up = jnp.mean(upstream, axis=-1, keepdims=True)
    mean_cross = jnp.mean(upstream * normed, axis=-1, keepdims=True)
    return inverse * (upstream - mean_up - normed * mean_cross)


def query_units(own_grid):
    lat_rows = own_grid.shape[1]
    lon_cols = own_grid.shape[2]
    channels = own_grid.shape[3]
    half_h = WH // 2
    half_w = WW // 2
    shaped = own_grid.reshape(LV, lat_rows // half_h, half_h, lon_cols // half_w, half_w, channels)
    return shaped.transpose(1, 3, 0, 2, 4, 5).reshape(
        lat_rows // half_h, lon_cols // half_w, LV * half_h * half_w, channels
    )


def query_layout(units):
    row_units = units.shape[0]
    col_units = units.shape[1]
    channels = units.shape[3]
    half_h = WH // 2
    half_w = WW // 2
    shaped = units.reshape(row_units, col_units, LV, half_h, half_w, channels)
    return shaped.transpose(2, 0, 3, 1, 4, 5).reshape(
        LV, row_units * half_h, col_units * half_w, channels
    )


def cross_rows(left_mat, right_mat):
    return lax.dot_general(
        left_mat, right_mat, (((0,), (0,)), ((), ())), preferred_element_type=jnp.float32
    )


def on_device(tokens, w_qkv, w_out, gain, tau, cotangent):
    lat_rows = tokens.shape[1]
    model_width = tokens.shape[3]
    head_count = tau.shape[0]
    head_dim = model_width // head_count
    half_h = WH // 2
    half_w = WW // 2
    tok_units = query_units(tokens)
    row_units, col_units, query_count = tok_units.shape[:3]
    assert row_units == 2 and col_units == 2
    tok_count = row_units * col_units * query_count
    tok_flat = tok_units.reshape(tok_count, model_width)
    cot_flat = query_units(cotangent).reshape(tok_count, model_width).astype(jnp.float32)
    weights_all = gather_rows_paired(jnp.concatenate([w_qkv, w_out], axis=1), "lon")
    w_qkv_all = weights_all[:, : 3 * model_width]
    w_out_all = weights_all[:, 3 * model_width :]
    projected = jnp.dot(tok_flat, w_qkv_all, preferred_element_type=jnp.float32)
    proj_b = projected.astype(jnp.bfloat16)
    query_f = proj_b[:, :model_width].astype(jnp.float32).reshape(tok_count, head_count, head_dim)
    key_f = (
        proj_b[:, model_width : 2 * model_width]
        .astype(jnp.float32)
        .reshape(tok_count, head_count, head_dim)
    )
    query_n, query_scale = unit_rows(query_f)
    key_n, key_scale = unit_rows(key_f)
    query_u = query_n.astype(jnp.bfloat16).reshape(row_units, col_units, query_count, model_width)
    key_b = key_n.astype(jnp.bfloat16).reshape(tok_count, model_width)
    kv_source = jnp.concatenate([key_b, proj_b[:, 2 * model_width :]], axis=1).reshape(
        row_units, col_units, query_count, 2 * model_width
    )
    ext_cols = with_halo(kv_source, (("lon", 1),), 1, True)
    ext_kv = with_halo(ext_cols, (("lat", 0),), 1, False)
    block = 16 * pl.cdiv(query_count, 16)
    ext_kv = jnp.pad(ext_kv, ((0, 0), (0, 0), (0, block - query_count), (0, 0)))
    level_win = (jnp.arange(block) // (half_h * half_w) + WL // 2) // WL
    same_level = (level_win[:query_count, None] == level_win[None, :]) & (
        jnp.arange(block) < query_count
    )
    block_row = jnp.arange(row_units + 2)
    first_row = lax.axis_index("lat") * lat_rows - half_h + half_h * block_row
    inside = (first_row >= 0) & (first_row < lat_rows * lax.axis_size("lat"))
    allowed = same_level[None, :, :] & inside[:, None, None]
    allowed = allowed.reshape(-1, 2, 1, query_count, block)
    allowed = jnp.broadcast_to(allowed, allowed.shape[:2] + (2, query_count, block))
    allowed = allowed.transpose(0, 3, 1, 2, 4).reshape(-1, query_count, 4 * block)
    allowed = allowed.astype(jnp.float32)
    mixed = window_fwd(tau, query_u, ext_kv, allowed)
    attended = mixed.astype(jnp.bfloat16).reshape(tok_count, model_width)
    y_rows = jnp.dot(attended, w_out_all, preferred_element_type=jnp.float32)
    normed, inverse = norm_forward(y_rows)
    output = (tok_flat.astype(jnp.float32) + gain * normed).astype(jnp.bfloat16)
    grad_y = norm_back(normed, inverse, gain * cot_flat).astype(jnp.bfloat16)
    grad_att = jnp.dot(grad_y, w_out_all.T, preferred_element_type=jnp.float32)
    grad_u = grad_att.astype(jnp.bfloat16).reshape(row_units, col_units, query_count, model_width)
    dquery, ext_grad = window_bwd(tau, query_u, ext_kv, grad_u, allowed)
    ext_grad = ext_grad[:, :, :query_count]
    grad_q = unit_back(
        query_f, query_scale, dquery.reshape(tok_count, head_count, head_dim)
    ).reshape(tok_count, model_width)
    north_rim = ext_grad[:1]
    south_rim = ext_grad[row_units + 1 :]
    rows = ext_grad[1 : row_units + 1]
    from_south = from_behind_2(north_rim.astype(jnp.bfloat16), "lat", -1).astype(north_rim.dtype)
    from_north = from_behind_2(south_rim.astype(jnp.bfloat16), "lat", 1).astype(south_rim.dtype)
    rows = rows.at[:1].add(from_north).at[row_units - 1 :].add(from_south)
    west_rim = rows[:, :1]
    east_rim = rows[:, col_units + 1 :]
    middle = rows[:, 1 : col_units + 1]
    from_east = from_behind(west_rim.astype(jnp.bfloat16), "lon", -1).astype(west_rim.dtype)
    from_west = from_behind(east_rim.astype(jnp.bfloat16), "lon", 1).astype(east_rim.dtype)
    middle = middle.at[:, :1].add(from_west).at[:, col_units - 1 :].add(from_east)
    own_grads = middle.reshape(tok_count, 2 * model_width)
    grad_k = unit_back(
        key_f, key_scale, own_grads[:, :model_width].reshape(tok_count, head_count, head_dim)
    ).reshape(tok_count, model_width)
    dvalue_src = own_grads[:, model_width:]
    grad_proj = jnp.concatenate([grad_q, grad_k, dvalue_src], axis=1).astype(jnp.bfloat16)
    grad_in = jnp.dot(grad_proj, w_qkv_all.T, preferred_element_type=jnp.float32)
    grad_tok = (cot_flat + grad_in).astype(jnp.bfloat16)
    partial = jnp.concatenate(
        [cross_rows(tok_flat, grad_proj), cross_rows(attended, grad_y)], axis=1
    ).astype(jnp.bfloat16)
    shard_sum = sum_rows_paired(partial, "lon")
    summed = sum_everywhere(shard_sum, "lat").astype(jnp.float32)
    grad_qkv = summed[:, : 3 * model_width]
    grad_out = summed[:, 3 * model_width :]
    unit_shape = (row_units, col_units, query_count, model_width)
    output = query_layout(output.reshape(unit_shape))
    grad_tokens = query_layout(grad_tok.reshape(unit_shape))
    return (output, grad_tokens, grad_qkv, grad_out)


def solution(mesh):
    in_specs = (
        P(None, "lat", "lon", None),
        P("lon", None),
        P("lon", None),
        P(),
        P(),
        P(None, "lat", "lon", None),
    )
    out_specs = (
        P(None, "lat", "lon", None),
        P(None, "lat", "lon", None),
        P("lon", None),
        P("lon", None),
    )
    return jax.shard_map(
        on_device, mesh=mesh, in_specs=in_specs, out_specs=out_specs, check_vma=False
    )
```

```python
import jax
import jax.numpy as jnp
from jax import lax
from jax.sharding import PartitionSpec as P
from jax.experimental import pallas as pl
from jax.experimental.pallas import tpu as pltpu

LV = 4
WL = 2
WH = 6
WW = 12
KEYS = 288


NORM_EPS = 1e-05
UNIT_EPS = 1e-06
HEADS_K = 8
HD_K = 64


def _nt(a, b):
    return lax.dot_general(a, b, (((1,), (1,)), ((), ())), preferred_element_type=jnp.float32)


def _tn(a, b):
    return lax.dot_general(a, b, (((0,), (0,)), ((), ())), preferred_element_type=jnp.float32)


def _window_probs(tau, query, keys, mask):
    scores = _nt(query, keys) * tau
    weights = jnp.exp(scores) * mask
    return weights / jnp.sum(weights, axis=-1, keepdims=True)


def _pair_lanes(pair, width=0):
    return pl.ds(width + 2 * pair * HD_K, 2 * HD_K)


def _pair_keys(kv_ref, lanes):
    rows, cols, block = kv_ref.shape[:3]
    return kv_ref[:, :, :, lanes].reshape(rows * cols * block, 2 * HD_K)


def _split_pair(block, low):
    zero = jnp.zeros_like(block)
    return jnp.where(low, block, zero), jnp.where(low, zero, block)


def attn_fwd_kernel(tau_ref, q_ref, kv_ref, mask_ref, out_ref):
    width = q_ref.shape[3]
    mask = mask_ref[0]
    for pair in range(HEADS_K // 2):
        lanes, value_lanes = _pair_lanes(pair), _pair_lanes(pair, width)
        query = q_ref[0, 0, :, lanes]
        low = lax.broadcasted_iota(jnp.int32, query.shape, 1) < HD_K
        keys = _pair_keys(kv_ref, lanes)
        values = _pair_keys(kv_ref, value_lanes)
        mixed = []
        for half, part in enumerate(_split_pair(query, low)):
            probs = _window_probs(tau_ref[2 * pair + half], part, keys, mask)
            mixed.append(
                jnp.dot(probs.astype(jnp.bfloat16), values, preferred_element_type=jnp.float32)
            )
        out_ref[0, 0, :, lanes] = jnp.where(low, mixed[0], mixed[1])


def attn_bwd_kernel(tau_ref, q_ref, kv_ref, g_ref, mask_ref, dq_ref, dkv_ref):
    width = q_ref.shape[3]
    mask = mask_ref[0]
    for pair in range(HEADS_K // 2):
        lanes, value_lanes = _pair_lanes(pair), _pair_lanes(pair, width)
        query = q_ref[0, 0, :, lanes]
        grad = g_ref[0, 0, :, lanes]
        low = lax.broadcasted_iota(jnp.int32, query.shape, 1) < HD_K
        keys = _pair_keys(kv_ref, lanes)
        values = _pair_keys(kv_ref, value_lanes)
        queries = _split_pair(query, low)
        grads = _split_pair(grad, low)
        dq, dk, dv = [], [], []
        for half in range(2):
            tau = tau_ref[2 * pair + half]
            probs = _window_probs(tau, queries[half], keys, mask)
            dprob = _nt(grads[half], values)
            total = jnp.sum(probs * dprob, axis=-1, keepdims=True)
            dscore = (tau * (probs * (dprob - total))).astype(jnp.bfloat16)
            dq.append(jnp.dot(dscore, keys, preferred_element_type=jnp.float32))
            dk.append(_tn(dscore, query))
            dv.append(_tn(probs.astype(jnp.bfloat16), grad))
        dq_ref[0, 0, :, lanes] = jnp.where(low, dq[0], dq[1])
        key_low = lax.broadcasted_iota(jnp.int32, keys.shape, 1) < HD_K
        out_shape = dkv_ref.shape[:3] + (2 * HD_K,)
        dkv_ref[:, :, :, lanes] = jnp.where(key_low, dk[0], dk[1]).reshape(out_shape)
        dkv_ref[:, :, :, value_lanes] = jnp.where(key_low, dv[0], dv[1]).reshape(out_shape)


def _window_of(i, j):
    return ((i + 1) // 2, (j + 1) // 2, 0, 0)


def window_fwd(tau, query, ext_kv, mask):
    row_units, col_units, queries, width = query.shape
    block = ext_kv.shape[2]
    return pl.pallas_call(
        attn_fwd_kernel,
        grid=(row_units, col_units),
        in_specs=[
            pl.BlockSpec(memory_space=pltpu.SMEM),
            pl.BlockSpec((1, 1, queries, width), lambda i, j: (i, j, 0, 0)),
            pl.BlockSpec((2, 2, block, 2 * width), _window_of),
            pl.BlockSpec((1, queries, mask.shape[2]), lambda i, j: ((i + 1) // 2, 0, 0)),
        ],
        out_specs=pl.BlockSpec((1, 1, queries, width), lambda i, j: (i, j, 0, 0)),
        out_shape=jax.ShapeDtypeStruct(query.shape, jnp.float32),
    )(tau, query, ext_kv, mask)


def window_bwd(tau, query, ext_kv, grad, mask):
    row_units, col_units, queries, width = query.shape
    block = ext_kv.shape[2]
    return pl.pallas_call(
        attn_bwd_kernel,
        grid=(row_units, col_units),
        in_specs=[
            pl.BlockSpec(memory_space=pltpu.SMEM),
            pl.BlockSpec((1, 1, queries, width), lambda i, j: (i, j, 0, 0)),
            pl.BlockSpec((2, 2, block, 2 * width), _window_of),
            pl.BlockSpec((1, 1, queries, width), lambda i, j: (i, j, 0, 0)),
            pl.BlockSpec((1, queries, mask.shape[2]), lambda i, j: ((i + 1) // 2, 0, 0)),
        ],
        out_specs=[
            pl.BlockSpec((1, 1, queries, width), lambda i, j: (i, j, 0, 0)),
            pl.BlockSpec((2, 2, block, 2 * width), _window_of),
        ],
        out_shape=[
            jax.ShapeDtypeStruct(query.shape, jnp.float32),
            jax.ShapeDtypeStruct(ext_kv.shape, jnp.float32),
        ],
    )(tau, query, ext_kv, grad, mask)


def with_halo(shard, sides, width, wrap):
    for axis, dim in sides:
        peers, length = (lax.axis_size(axis), shard.shape[dim])
        up = [(i, (i + 1) % peers) for i in range(peers if wrap else peers - 1)]
        down = [(j, i) for i, j in up]
        last = lax.slice_in_dim(shard, length - width, length, axis=dim)
        initial = lax.slice_in_dim(shard, 0, width, axis=dim)
        before = lax.ppermute(last, axis, up)
        after = lax.ppermute(initial, axis, down)
        shard = jnp.concatenate([before, shard, after], axis=dim)
    return shard


def from_behind(block, axis, distance):
    devices = range(lax.axis_size(axis))
    route = [((i - distance) % len(devices), i) for i in devices]
    return lax.ppermute(block, axis, route)


def from_behind_2(block, axis, distance):
    devices = range(lax.axis_size(axis))
    route = [(i - distance, i) for i in devices if i - distance in devices]
    return lax.ppermute(block, axis, route)


def gather_rows(block, axis):
    peers = lax.axis_size(axis)
    copies = jnp.broadcast_to(block[None], (peers,) + block.shape)
    spread = lax.all_to_all(copies, axis, 0, 0, tiled=False)
    return spread.reshape((peers * block.shape[0],) + block.shape[1:])


def sum_rows(partial, axis):
    peers = lax.axis_size(axis)
    chunks = partial.reshape((peers, partial.shape[0] // peers) + partial.shape[1:])
    spread = lax.all_to_all(chunks, axis, 0, 0, tiled=False)
    return jnp.sum(spread.astype(jnp.float32), axis=0)


def sum_everywhere(partial, axis):
    peers = lax.axis_size(axis)
    own = sum_rows(partial, axis).astype(jnp.bfloat16)
    copies = jnp.broadcast_to(own[None], (peers,) + own.shape)
    spread = lax.all_to_all(copies, axis, 0, 0, tiled=False)
    return spread.reshape((peers * own.shape[0],) + own.shape[1:])


def chip_partner(block):
    peers = lax.axis_size("lat")
    return lax.ppermute(block, "lat", [(i, i ^ 1) for i in range(peers)])


def gather_rows_paired(block, axis):
    core = lax.axis_index("lat") % 2
    halves = block.reshape(block.shape[0], 2, block.shape[1] // 2)
    mine = lax.dynamic_index_in_dim(halves, core, axis=1, keepdims=False)
    gathered = gather_rows(mine, axis)
    other = chip_partner(gathered)
    return jnp.where(
        core == 0,
        jnp.concatenate([gathered, other], axis=1),
        jnp.concatenate([other, gathered], axis=1),
    )


def sum_rows_paired(partial, axis):
    peers = lax.axis_size(axis)
    core = lax.axis_index("lat") % 2
    blocks = partial.reshape(peers, 2, partial.shape[0] // (2 * peers), partial.shape[1])
    keep = lax.dynamic_index_in_dim(blocks, core, axis=1, keepdims=False)
    give = lax.dynamic_index_in_dim(blocks, 1 - core, axis=1, keepdims=False)
    pair = keep.astype(jnp.float32) + chip_partner(give).astype(jnp.float32)
    return sum_rows(pair.astype(jnp.bfloat16).reshape(-1, partial.shape[1]), axis)


def sum_lat_paired(own):
    peers = lax.axis_size("lat")
    total = own
    bit = 2
    while bit < peers:
        sent = total.astype(jnp.bfloat16)
        got = lax.ppermute(sent, "lat", [(i, i ^ bit) for i in range(peers)])
        total = sent.astype(jnp.float32) + got.astype(jnp.float32)
        bit *= 2
    final = total.astype(jnp.bfloat16)
    other = chip_partner(final)
    core = lax.axis_index("lat") % 2
    return jnp.where(
        core == 0,
        jnp.concatenate([final, other], axis=0),
        jnp.concatenate([other, final], axis=0),
    )


def unit_rows(vectors):
    scaling = lax.rsqrt(jnp.sum(vectors * vectors, axis=-1, keepdims=True) + UNIT_EPS)
    return (vectors * scaling, scaling)


def unit_back(vectors, scaling, gradient):
    inner_sum = jnp.sum(vectors * gradient, axis=-1, keepdims=True)
    return scaling * (gradient - vectors * (inner_sum * scaling * scaling))


def norm_forward(y_rows):
    centered = y_rows - jnp.mean(y_rows, axis=-1, keepdims=True)
    inverse = lax.rsqrt(jnp.mean(centered * centered, axis=-1, keepdims=True) + NORM_EPS)
    return (centered * inverse, inverse)


def norm_back(normed, inverse, upstream):
    mean_up = jnp.mean(upstream, axis=-1, keepdims=True)
    mean_cross = jnp.mean(upstream * normed, axis=-1, keepdims=True)
    return inverse * (upstream - mean_up - normed * mean_cross)


def query_units(own_grid):
    lat_rows = own_grid.shape[1]
    lon_cols = own_grid.shape[2]
    channels = own_grid.shape[3]
    half_h = WH // 2
    half_w = WW // 2
    shaped = own_grid.reshape(LV, lat_rows // half_h, half_h, lon_cols // half_w, half_w, channels)
    return shaped.transpose(1, 3, 0, 2, 4, 5).reshape(
        lat_rows // half_h, lon_cols // half_w, LV * half_h * half_w, channels
    )


def query_layout(units):
    row_units = units.shape[0]
    col_units = units.shape[1]
    channels = units.shape[3]
    half_h = WH // 2
    half_w = WW // 2
    shaped = units.reshape(row_units, col_units, LV, half_h, half_w, channels)
    return shaped.transpose(2, 0, 3, 1, 4, 5).reshape(
        LV, row_units * half_h, col_units * half_w, channels
    )


def cross_rows(left_mat, right_mat):
    return lax.dot_general(
        left_mat, right_mat, (((0,), (0,)), ((), ())), preferred_element_type=jnp.float32
    )


def on_device(tokens, w_qkv, w_out, gain, tau, cotangent):
    lat_rows = tokens.shape[1]
    model_width = tokens.shape[3]
    head_count = tau.shape[0]
    head_dim = model_width // head_count
    half_h = WH // 2
    half_w = WW // 2
    tok_units = query_units(tokens)
    row_units, col_units, query_count = tok_units.shape[:3]
    assert row_units == 2 and col_units == 2
    tok_count = row_units * col_units * query_count
    tok_flat = tok_units.reshape(tok_count, model_width)
    cot_flat = query_units(cotangent).reshape(tok_count, model_width).astype(jnp.float32)
    weights_all = gather_rows_paired(jnp.concatenate([w_qkv, w_out], axis=1), "lon")
    w_qkv_all = weights_all[:, : 3 * model_width]
    w_out_all = weights_all[:, 3 * model_width :]
    projected = jnp.dot(tok_flat, w_qkv_all, preferred_element_type=jnp.float32)
    proj_b = projected.astype(jnp.bfloat16)
    query_f = proj_b[:, :model_width].astype(jnp.float32).reshape(tok_count, head_count, head_dim)
    key_f = (
        proj_b[:, model_width : 2 * model_width]
        .astype(jnp.float32)
        .reshape(tok_count, head_count, head_dim)
    )
    query_n, query_scale = unit_rows(query_f)
    key_n, key_scale = unit_rows(key_f)
    query_u = query_n.astype(jnp.bfloat16).reshape(row_units, col_units, query_count, model_width)
    key_b = key_n.astype(jnp.bfloat16).reshape(tok_count, model_width)
    kv_source = jnp.concatenate([key_b, proj_b[:, 2 * model_width :]], axis=1).reshape(
        row_units, col_units, query_count, 2 * model_width
    )
    ext_cols = with_halo(kv_source, (("lon", 1),), 1, True)
    ext_kv = with_halo(ext_cols, (("lat", 0),), 1, False)
    block = 16 * pl.cdiv(query_count, 16)
    ext_kv = jnp.pad(ext_kv, ((0, 0), (0, 0), (0, block - query_count), (0, 0)))
    level_win = (jnp.arange(block) // (half_h * half_w) + WL // 2) // WL
    same_level = (level_win[:query_count, None] == level_win[None, :]) & (
        jnp.arange(block) < query_count
    )
    block_row = jnp.arange(row_units + 2)
    first_row = lax.axis_index("lat") * lat_rows - half_h + half_h * block_row
    inside = (first_row >= 0) & (first_row < lat_rows * lax.axis_size("lat"))
    allowed = same_level[None, :, :] & inside[:, None, None]
    allowed = allowed.reshape(-1, 2, 1, query_count, block)
    allowed = jnp.broadcast_to(allowed, allowed.shape[:2] + (2, query_count, block))
    allowed = allowed.transpose(0, 3, 1, 2, 4).reshape(-1, query_count, 4 * block)
    allowed = allowed.astype(jnp.float32)
    mixed = window_fwd(tau, query_u, ext_kv, allowed)
    attended = mixed.astype(jnp.bfloat16).reshape(tok_count, model_width)
    y_rows = jnp.dot(attended, w_out_all, preferred_element_type=jnp.float32)
    normed, inverse = norm_forward(y_rows)
    output = (tok_flat.astype(jnp.float32) + gain * normed).astype(jnp.bfloat16)
    grad_y = norm_back(normed, inverse, gain * cot_flat).astype(jnp.bfloat16)
    grad_att = jnp.dot(grad_y, w_out_all.T, preferred_element_type=jnp.float32)
    grad_u = grad_att.astype(jnp.bfloat16).reshape(row_units, col_units, query_count, model_width)
    dquery, ext_grad = window_bwd(tau, query_u, ext_kv, grad_u, allowed)
    ext_grad = ext_grad[:, :, :query_count]
    grad_q = unit_back(
        query_f, query_scale, dquery.reshape(tok_count, head_count, head_dim)
    ).reshape(tok_count, model_width)
    north_rim = ext_grad[:1]
    south_rim = ext_grad[row_units + 1 :]
    rows = ext_grad[1 : row_units + 1]
    from_south = from_behind_2(north_rim.astype(jnp.bfloat16), "lat", -1).astype(north_rim.dtype)
    from_north = from_behind_2(south_rim.astype(jnp.bfloat16), "lat", 1).astype(south_rim.dtype)
    rows = rows.at[:1].add(from_north).at[row_units - 1 :].add(from_south)
    west_rim = rows[:, :1]
    east_rim = rows[:, col_units + 1 :]
    middle = rows[:, 1 : col_units + 1]
    from_east = from_behind(west_rim.astype(jnp.bfloat16), "lon", -1).astype(west_rim.dtype)
    from_west = from_behind(east_rim.astype(jnp.bfloat16), "lon", 1).astype(east_rim.dtype)
    middle = middle.at[:, :1].add(from_west).at[:, col_units - 1 :].add(from_east)
    own_grads = middle.reshape(tok_count, 2 * model_width)
    grad_k = unit_back(
        key_f, key_scale, own_grads[:, :model_width].reshape(tok_count, head_count, head_dim)
    ).reshape(tok_count, model_width)
    dvalue_src = own_grads[:, model_width:]
    grad_proj = jnp.concatenate([grad_q, grad_k, dvalue_src], axis=1).astype(jnp.bfloat16)
    grad_in = jnp.dot(grad_proj, w_qkv_all.T, preferred_element_type=jnp.float32)
    grad_tok = (cot_flat + grad_in).astype(jnp.bfloat16)
    partial = jnp.concatenate(
        [cross_rows(tok_flat, grad_proj), cross_rows(attended, grad_y)], axis=1
    ).astype(jnp.bfloat16)
    shard_sum = sum_rows_paired(partial, "lon")
    summed = sum_lat_paired(shard_sum).astype(jnp.float32)
    grad_qkv = summed[:, : 3 * model_width]
    grad_out = summed[:, 3 * model_width :]
    unit_shape = (row_units, col_units, query_count, model_width)
    output = query_layout(output.reshape(unit_shape))
    grad_tokens = query_layout(grad_tok.reshape(unit_shape))
    return (output, grad_tokens, grad_qkv, grad_out)


def solution(mesh):
    in_specs = (
        P(None, "lat", "lon", None),
        P("lon", None),
        P("lon", None),
        P(),
        P(),
        P(None, "lat", "lon", None),
    )
    out_specs = (
        P(None, "lat", "lon", None),
        P(None, "lat", "lon", None),
        P("lon", None),
        P("lon", None),
    )
    return jax.shard_map(
        on_device, mesh=mesh, in_specs=in_specs, out_specs=out_specs, check_vma=False
    )
```

```python
import jax
import jax.numpy as jnp
from jax import lax
from jax.sharding import PartitionSpec as P
from jax.experimental import pallas as pl
from jax.experimental.pallas import tpu as pltpu

LV = 4
WL = 2
WH = 6
WW = 12
KEYS = 288


NORM_EPS = 1e-05
UNIT_EPS = 1e-06
HEADS_K = 8
HD_K = 64


def _nt(a, b):
    return lax.dot_general(a, b, (((1,), (1,)), ((), ())), preferred_element_type=jnp.float32)


def _tn(a, b):
    return lax.dot_general(a, b, (((0,), (0,)), ((), ())), preferred_element_type=jnp.float32)


def _window_probs(tau, query, keys, mask):
    scores = _nt(query, keys) * tau
    weights = jnp.exp(scores) * mask
    return weights / jnp.sum(weights, axis=-1, keepdims=True)


def _pair_lanes(pair, width=0):
    return pl.ds(width + 2 * pair * HD_K, 2 * HD_K)


def _pair_keys(kv_ref, lanes):
    rows, cols, block = kv_ref.shape[:3]
    return kv_ref[:, :, :, lanes].reshape(rows * cols * block, 2 * HD_K)


def _split_pair(block, low):
    zero = jnp.zeros_like(block)
    return jnp.where(low, block, zero), jnp.where(low, zero, block)


def attn_fwd_kernel(tau_ref, q_ref, kv_ref, mask_ref, out_ref):
    width = q_ref.shape[3]
    mask = mask_ref[0]
    for pair in range(HEADS_K // 2):
        lanes, value_lanes = _pair_lanes(pair), _pair_lanes(pair, width)
        query = q_ref[0, 0, :, lanes]
        low = lax.broadcasted_iota(jnp.int32, query.shape, 1) < HD_K
        keys = _pair_keys(kv_ref, lanes)
        values = _pair_keys(kv_ref, value_lanes)
        mixed = []
        for half, part in enumerate(_split_pair(query, low)):
            probs = _window_probs(tau_ref[2 * pair + half], part, keys, mask)
            mixed.append(
                jnp.dot(probs.astype(jnp.bfloat16), values, preferred_element_type=jnp.float32)
            )
        out_ref[0, 0, :, lanes] = jnp.where(low, mixed[0], mixed[1]).astype(out_ref.dtype)


def attn_bwd_kernel(tau_ref, q_ref, kv_ref, g_ref, mask_ref, dq_ref, dkv_ref):
    width = q_ref.shape[3]
    mask = mask_ref[0]
    for pair in range(HEADS_K // 2):
        lanes, value_lanes = _pair_lanes(pair), _pair_lanes(pair, width)
        query = q_ref[0, 0, :, lanes]
        grad = g_ref[0, 0, :, lanes]
        low = lax.broadcasted_iota(jnp.int32, query.shape, 1) < HD_K
        keys = _pair_keys(kv_ref, lanes)
        values = _pair_keys(kv_ref, value_lanes)
        queries = _split_pair(query, low)
        grads = _split_pair(grad, low)
        dq, dk, dv = [], [], []
        for half in range(2):
            tau = tau_ref[2 * pair + half]
            probs = _window_probs(tau, queries[half], keys, mask)
            dprob = _nt(grads[half], values)
            total = jnp.sum(probs * dprob, axis=-1, keepdims=True)
            dscore = (tau * (probs * (dprob - total))).astype(jnp.bfloat16)
            dq.append(jnp.dot(dscore, keys, preferred_element_type=jnp.float32))
            dk.append(_tn(dscore, query))
            dv.append(_tn(probs.astype(jnp.bfloat16), grad))
        dq_ref[0, 0, :, lanes] = jnp.where(low, dq[0], dq[1])
        key_low = lax.broadcasted_iota(jnp.int32, keys.shape, 1) < HD_K
        out_shape = dkv_ref.shape[:3] + (2 * HD_K,)
        dkv_ref[:, :, :, lanes] = jnp.where(key_low, dk[0], dk[1]).reshape(out_shape)
        dkv_ref[:, :, :, value_lanes] = jnp.where(key_low, dv[0], dv[1]).reshape(out_shape)


def _window_of(i, j):
    return ((i + 1) // 2, (j + 1) // 2, 0, 0)


def window_fwd(tau, query, ext_kv, mask):
    row_units, col_units, queries, width = query.shape
    block = ext_kv.shape[2]
    return pl.pallas_call(
        attn_fwd_kernel,
        grid=(row_units, col_units),
        in_specs=[
            pl.BlockSpec(memory_space=pltpu.SMEM),
            pl.BlockSpec((1, 1, queries, width), lambda i, j: (i, j, 0, 0)),
            pl.BlockSpec((2, 2, block, 2 * width), _window_of),
            pl.BlockSpec((1, queries, mask.shape[2]), lambda i, j: ((i + 1) // 2, 0, 0)),
        ],
        out_specs=pl.BlockSpec((1, 1, queries, width), lambda i, j: (i, j, 0, 0)),
        out_shape=jax.ShapeDtypeStruct(query.shape, jnp.bfloat16),
    )(tau, query, ext_kv, mask)


def window_bwd(tau, query, ext_kv, grad, mask):
    row_units, col_units, queries, width = query.shape
    block = ext_kv.shape[2]
    return pl.pallas_call(
        attn_bwd_kernel,
        grid=(row_units, col_units),
        in_specs=[
            pl.BlockSpec(memory_space=pltpu.SMEM),
            pl.BlockSpec((1, 1, queries, width), lambda i, j: (i, j, 0, 0)),
            pl.BlockSpec((2, 2, block, 2 * width), _window_of),
            pl.BlockSpec((1, 1, queries, width), lambda i, j: (i, j, 0, 0)),
            pl.BlockSpec((1, queries, mask.shape[2]), lambda i, j: ((i + 1) // 2, 0, 0)),
        ],
        out_specs=[
            pl.BlockSpec((1, 1, queries, width), lambda i, j: (i, j, 0, 0)),
            pl.BlockSpec((2, 2, block, 2 * width), _window_of),
        ],
        out_shape=[
            jax.ShapeDtypeStruct(query.shape, jnp.float32),
            jax.ShapeDtypeStruct(ext_kv.shape, jnp.float32),
        ],
    )(tau, query, ext_kv, grad, mask)


def with_halo(shard, sides, width, wrap):
    for axis, dim in sides:
        peers, length = (lax.axis_size(axis), shard.shape[dim])
        up = [(i, (i + 1) % peers) for i in range(peers if wrap else peers - 1)]
        down = [(j, i) for i, j in up]
        last = lax.slice_in_dim(shard, length - width, length, axis=dim)
        initial = lax.slice_in_dim(shard, 0, width, axis=dim)
        before = lax.ppermute(last, axis, up)
        after = lax.ppermute(initial, axis, down)
        shard = jnp.concatenate([before, shard, after], axis=dim)
    return shard


def from_behind(block, axis, distance):
    devices = range(lax.axis_size(axis))
    route = [((i - distance) % len(devices), i) for i in devices]
    return lax.ppermute(block, axis, route)


def from_behind_2(block, axis, distance):
    devices = range(lax.axis_size(axis))
    route = [(i - distance, i) for i in devices if i - distance in devices]
    return lax.ppermute(block, axis, route)


def gather_rows(block, axis):
    peers = lax.axis_size(axis)
    copies = jnp.broadcast_to(block[None], (peers,) + block.shape)
    spread = lax.all_to_all(copies, axis, 0, 0, tiled=False)
    return spread.reshape((peers * block.shape[0],) + block.shape[1:])


def sum_rows(partial, axis):
    peers = lax.axis_size(axis)
    chunks = partial.reshape((peers, partial.shape[0] // peers) + partial.shape[1:])
    spread = lax.all_to_all(chunks, axis, 0, 0, tiled=False)
    return jnp.sum(spread.astype(jnp.float32), axis=0)


def sum_everywhere(partial, axis):
    peers = lax.axis_size(axis)
    own = sum_rows(partial, axis).astype(jnp.bfloat16)
    copies = jnp.broadcast_to(own[None], (peers,) + own.shape)
    spread = lax.all_to_all(copies, axis, 0, 0, tiled=False)
    return spread.reshape((peers * own.shape[0],) + own.shape[1:])


def chip_partner(block):
    peers = lax.axis_size("lat")
    return lax.ppermute(block, "lat", [(i, i ^ 1) for i in range(peers)])


def gather_rows_paired(block, axis):
    core = lax.axis_index("lat") % 2
    halves = block.reshape(block.shape[0], 2, block.shape[1] // 2)
    mine = lax.dynamic_index_in_dim(halves, core, axis=1, keepdims=False)
    gathered = gather_rows(mine, axis)
    other = chip_partner(gathered)
    return jnp.where(
        core == 0,
        jnp.concatenate([gathered, other], axis=1),
        jnp.concatenate([other, gathered], axis=1),
    )


def sum_rows_paired(partial, axis):
    peers = lax.axis_size(axis)
    core = lax.axis_index("lat") % 2
    blocks = partial.reshape(peers, 2, partial.shape[0] // (2 * peers), partial.shape[1])
    keep = lax.dynamic_index_in_dim(blocks, core, axis=1, keepdims=False)
    give = lax.dynamic_index_in_dim(blocks, 1 - core, axis=1, keepdims=False)
    pair = keep.astype(jnp.float32) + chip_partner(give).astype(jnp.float32)
    return sum_rows(pair.astype(jnp.bfloat16).reshape(-1, partial.shape[1]), axis)


def sum_lat_paired(own):
    peers = lax.axis_size("lat")
    total = own
    bit = 2
    while bit < peers:
        sent = total.astype(jnp.bfloat16)
        got = lax.ppermute(sent, "lat", [(i, i ^ bit) for i in range(peers)])
        total = sent.astype(jnp.float32) + got.astype(jnp.float32)
        bit *= 2
    final = total.astype(jnp.bfloat16)
    other = chip_partner(final)
    core = lax.axis_index("lat") % 2
    return jnp.where(
        core == 0,
        jnp.concatenate([final, other], axis=0),
        jnp.concatenate([other, final], axis=0),
    )


def unit_rows(vectors):
    scaling = lax.rsqrt(jnp.sum(vectors * vectors, axis=-1, keepdims=True) + UNIT_EPS)
    return (vectors * scaling, scaling)


def unit_back(vectors, scaling, gradient):
    inner_sum = jnp.sum(vectors * gradient, axis=-1, keepdims=True)
    return scaling * (gradient - vectors * (inner_sum * scaling * scaling))


def norm_forward(y_rows):
    centered = y_rows - jnp.mean(y_rows, axis=-1, keepdims=True)
    inverse = lax.rsqrt(jnp.mean(centered * centered, axis=-1, keepdims=True) + NORM_EPS)
    return (centered * inverse, inverse)


def norm_back(normed, inverse, upstream):
    mean_up = jnp.mean(upstream, axis=-1, keepdims=True)
    mean_cross = jnp.mean(upstream * normed, axis=-1, keepdims=True)
    return inverse * (upstream - mean_up - normed * mean_cross)


def query_units(own_grid):
    lat_rows = own_grid.shape[1]
    lon_cols = own_grid.shape[2]
    channels = own_grid.shape[3]
    half_h = WH // 2
    half_w = WW // 2
    shaped = own_grid.reshape(LV, lat_rows // half_h, half_h, lon_cols // half_w, half_w, channels)
    return shaped.transpose(1, 3, 0, 2, 4, 5).reshape(
        lat_rows // half_h, lon_cols // half_w, LV * half_h * half_w, channels
    )


def query_layout(units):
    row_units = units.shape[0]
    col_units = units.shape[1]
    channels = units.shape[3]
    half_h = WH // 2
    half_w = WW // 2
    shaped = units.reshape(row_units, col_units, LV, half_h, half_w, channels)
    return shaped.transpose(2, 0, 3, 1, 4, 5).reshape(
        LV, row_units * half_h, col_units * half_w, channels
    )


def cross_rows(left_mat, right_mat):
    return lax.dot_general(
        left_mat, right_mat, (((0,), (0,)), ((), ())), preferred_element_type=jnp.float32
    )


def on_device(tokens, w_qkv, w_out, gain, tau, cotangent):
    lat_rows = tokens.shape[1]
    model_width = tokens.shape[3]
    head_count = tau.shape[0]
    head_dim = model_width // head_count
    half_h = WH // 2
    half_w = WW // 2
    tok_units = query_units(tokens)
    row_units, col_units, query_count = tok_units.shape[:3]
    assert row_units == 2 and col_units == 2
    tok_count = row_units * col_units * query_count
    tok_flat = tok_units.reshape(tok_count, model_width)
    cot_flat = query_units(cotangent).reshape(tok_count, model_width).astype(jnp.float32)
    weights_all = gather_rows_paired(jnp.concatenate([w_qkv, w_out], axis=1), "lon")
    w_qkv_all = weights_all[:, : 3 * model_width]
    w_out_all = weights_all[:, 3 * model_width :]
    projected = jnp.dot(tok_flat, w_qkv_all, preferred_element_type=jnp.float32)
    proj_b = projected.astype(jnp.bfloat16)
    query_f = proj_b[:, :model_width].astype(jnp.float32).reshape(tok_count, head_count, head_dim)
    key_f = (
        proj_b[:, model_width : 2 * model_width]
        .astype(jnp.float32)
        .reshape(tok_count, head_count, head_dim)
    )
    query_n, query_scale = unit_rows(query_f)
    key_n, key_scale = unit_rows(key_f)
    query_u = query_n.astype(jnp.bfloat16).reshape(row_units, col_units, query_count, model_width)
    key_b = key_n.astype(jnp.bfloat16).reshape(tok_count, model_width)
    kv_source = jnp.concatenate([key_b, proj_b[:, 2 * model_width :]], axis=1).reshape(
        row_units, col_units, query_count, 2 * model_width
    )
    ext_cols = with_halo(kv_source, (("lon", 1),), 1, True)
    ext_kv = with_halo(ext_cols, (("lat", 0),), 1, False)
    block = 16 * pl.cdiv(query_count, 16)
    ext_kv = jnp.pad(ext_kv, ((0, 0), (0, 0), (0, block - query_count), (0, 0)))
    level_win = (jnp.arange(block) // (half_h * half_w) + WL // 2) // WL
    same_level = (level_win[:query_count, None] == level_win[None, :]) & (
        jnp.arange(block) < query_count
    )
    block_row = jnp.arange(row_units + 2)
    first_row = lax.axis_index("lat") * lat_rows - half_h + half_h * block_row
    inside = (first_row >= 0) & (first_row < lat_rows * lax.axis_size("lat"))
    allowed = same_level[None, :, :] & inside[:, None, None]
    allowed = allowed.reshape(-1, 2, 1, query_count, block)
    allowed = jnp.broadcast_to(allowed, allowed.shape[:2] + (2, query_count, block))
    allowed = allowed.transpose(0, 3, 1, 2, 4).reshape(-1, query_count, 4 * block)
    allowed = allowed.astype(jnp.float32)
    mixed = window_fwd(tau, query_u, ext_kv, allowed)
    attended = mixed.reshape(tok_count, model_width)
    y_rows = jnp.dot(attended, w_out_all, preferred_element_type=jnp.float32)
    normed, inverse = norm_forward(y_rows)
    output = (tok_flat.astype(jnp.float32) + gain * normed).astype(jnp.bfloat16)
    grad_y = norm_back(normed, inverse, gain * cot_flat).astype(jnp.bfloat16)
    grad_att = jnp.dot(grad_y, w_out_all.T, preferred_element_type=jnp.float32)
    grad_u = grad_att.astype(jnp.bfloat16).reshape(row_units, col_units, query_count, model_width)
    dquery, ext_grad = window_bwd(tau, query_u, ext_kv, grad_u, allowed)
    ext_grad = ext_grad[:, :, :query_count]
    grad_q = unit_back(
        query_f, query_scale, dquery.reshape(tok_count, head_count, head_dim)
    ).reshape(tok_count, model_width)
    north_rim = ext_grad[:1]
    south_rim = ext_grad[row_units + 1 :]
    rows = ext_grad[1 : row_units + 1]
    from_south = from_behind_2(north_rim.astype(jnp.bfloat16), "lat", -1).astype(north_rim.dtype)
    from_north = from_behind_2(south_rim.astype(jnp.bfloat16), "lat", 1).astype(south_rim.dtype)
    rows = rows.at[:1].add(from_north).at[row_units - 1 :].add(from_south)
    west_rim = rows[:, :1]
    east_rim = rows[:, col_units + 1 :]
    middle = rows[:, 1 : col_units + 1]
    from_east = from_behind(west_rim.astype(jnp.bfloat16), "lon", -1).astype(west_rim.dtype)
    from_west = from_behind(east_rim.astype(jnp.bfloat16), "lon", 1).astype(east_rim.dtype)
    middle = middle.at[:, :1].add(from_west).at[:, col_units - 1 :].add(from_east)
    own_grads = middle.reshape(tok_count, 2 * model_width)
    grad_k = unit_back(
        key_f, key_scale, own_grads[:, :model_width].reshape(tok_count, head_count, head_dim)
    ).reshape(tok_count, model_width)
    dvalue_src = own_grads[:, model_width:]
    grad_proj = jnp.concatenate([grad_q, grad_k, dvalue_src], axis=1).astype(jnp.bfloat16)
    grad_in = jnp.dot(grad_proj, w_qkv_all.T, preferred_element_type=jnp.float32)
    grad_tok = (cot_flat + grad_in).astype(jnp.bfloat16)
    partial = jnp.concatenate(
        [cross_rows(tok_flat, grad_proj), cross_rows(attended, grad_y)], axis=1
    ).astype(jnp.bfloat16)
    shard_sum = sum_rows_paired(partial, "lon")
    summed = sum_lat_paired(shard_sum).astype(jnp.float32)
    grad_qkv = summed[:, : 3 * model_width]
    grad_out = summed[:, 3 * model_width :]
    unit_shape = (row_units, col_units, query_count, model_width)
    output = query_layout(output.reshape(unit_shape))
    grad_tokens = query_layout(grad_tok.reshape(unit_shape))
    return (output, grad_tokens, grad_qkv, grad_out)


def solution(mesh):
    in_specs = (
        P(None, "lat", "lon", None),
        P("lon", None),
        P("lon", None),
        P(),
        P(),
        P(None, "lat", "lon", None),
    )
    out_specs = (
        P(None, "lat", "lon", None),
        P(None, "lat", "lon", None),
        P("lon", None),
        P("lon", None),
    )
    return jax.shard_map(
        on_device, mesh=mesh, in_specs=in_specs, out_specs=out_specs, check_vma=False
    )
```
